32 devices in a mesh: space: 4 (over y, core), tm: 8 (over z, x).
Axes of the slice: x: 2, y: 2, z: 4, core: 2. Of those that a mesh axis runs over, the one named last changes fastest.
Arguments:
- probe_field: bfloat16 [4096, 2048], P('space', 'tm'), may hold values from -5 to 5
- kappa: float32 [4096], P('space'), may hold values from 0.1 to 1
- theta_space: float32 [32], P('tm'), may hold values from 0.3 to 1
- theta_time: float32 [32], P('tm'), may hold values from 0.2 to 0.8
- diag_blocks: bfloat16 [32, 128, 128], P('space'), may hold values from -0.05 to 1.05
- off_blocks: bfloat16 [32, 8, 128, 128], P('space'), may hold values from -0.375 to 0.375
- block_cols: int32 [32, 8], P('space'), may hold values from 0 to 11
- halo_needs: int32 [16], P('space'), may hold values from 0 to 7
- covariates: bfloat16 [65536, 256], P(('space', 'tm')), may hold values from -4 to 4
- obs_owner: int32 [65536, 1], P(('space', 'tm')), may hold values from 0 to 3; in each aligned block of 2048 rows (0 to 2047, 2048 to 4095, ...) at most 1024 rows name the same one
- obs_cell: int32 [65536], P(('space', 'tm')), may hold values from 0 to 4095
- svc_coef: bfloat16 [4096, 256], P('space'), may hold values from -0.375 to 0.375
Outputs:
- solution: float32 [4096, 2048], P('space', 'tm')
- grads: float32 [2, 2048], P(None, 'tm')
The draws below stay inside these ranges and needn't reach their ends.
Inputs may be any that keep to these rules, and one draw needn't show every extreme that they name: `obs_owner`: in each aligned block of 2048 rows (the rows of one device) no owner is named by more than 1024 rows, a bound that some block reaches.
All inputs are finite; a program needn't handle non-finite values.
Results may differ from the reference program's by a relative error of at most 0.0021.
Values may be sent and summed in bfloat16 or wider, within the bound.
No kernel may reach another device: no remote copies, remote signals or barrier semaphores. Data moves between devices by JAX's collectives and lax.ppermute only.
A program may use at most 64 MiB of HBM per device.

```python
import math
import jax
import jax.numpy as jnp
import numpy as np
from jax import lax

NB_DEV = 8
BLOCK = 128
NNZ_OFF = 8
HALO_B = 2
T_DEV = 4
PROBES = 64
NCOV = 256
OBS_DEV = 2048
ITERS = 4
CAP = 1024
NODES_DEV = 1024
NB = 32
NODES = 4096
NT = 32
OBS = 65536
NEEDS = 16
N_SPACE = 4
N_TM = 8


def draw_diag_blocks(key, part):
    shape = (NB, BLOCK, BLOCK)
    noise = jax.random.uniform(key, shape, jnp.float32, -0.04, 0.04)
    identity = jnp.eye(BLOCK, dtype=jnp.float32)[None, :, :]
    return (identity + noise).astype(jnp.bfloat16)


def plant(drawn, rng, smallest, top_value):
    place = [jax.random.randint(jax.random.fold_in(rng, axis), (), 0, length) for axis, length in enumerate(drawn.shape)]
    longest = drawn.shape.index(max(drawn.shape))
    beside = place[:longest] + [(place[longest] + 1) % drawn.shape[longest]] + place[longest + 1:]
    return drawn.at[tuple(place)].set(smallest).at[tuple(beside)].set(top_value)


def block_scale(rng, dims, cuts, smallest, high):
    factor_of = 1.0
    for dim, parts in cuts:
        steps = jax.random.uniform(jax.random.fold_in(jax.random.fold_in(rng, 6), dim), (parts,), jnp.float32, smallest / len(cuts), high / len(cuts))
        factor_of = factor_of * jnp.repeat(jnp.exp(steps), dims[dim] // parts).reshape((-1,) + (1,) * (len(dims) - 1 - dim))
    return factor_of


def routed_block(rng, own, number, rows, number_of, top, most, slope):
    ranking = jax.random.permutation(rng, number_of)
    crowded, common = shares(number_of, rows * top, most, slope, True), shares(number_of, rows * top, most, slope, False)
    places = jnp.arange(number_of)

    def named(lengths, offset_by):
        used = int((lengths > 0).sum())
        fixed = max(1, used // 4)
        shifted = fixed + (places - fixed + offset_by * (used - fixed)) % max(1, number_of - fixed)
        return jnp.zeros((number_of,), jnp.int32).at[ranking[jnp.where(places < fixed, places, shifted)]].set(jnp.asarray(lengths, jnp.int32))

    lengths = jnp.where(number % 4 == 0, named(crowded, number // 4), named(common, number - number // 4 - 1))
    mixed = jax.random.permutation(jax.random.fold_in(own, 3), number_of)
    giver, sink = mixed[0:number_of // 2 * 2:2], mixed[1:number_of // 2 * 2:2]
    slack = jnp.minimum(lengths[giver] - 1, most - lengths[sink]) // 2
    slack = jnp.where((giver == ranking[0]) | (sink == ranking[0]) | (lengths[sink] == 0), 0, jnp.maximum(slack, 0))
    shifted = jax.random.randint(jax.random.fold_in(own, 4), (number_of // 2,), 0, 1 << 20) % (slack + 1)
    lengths = lengths.at[giver].add(-shifted).at[sink].add(shifted)
    members = jnp.searchsorted(jnp.cumsum(lengths), jnp.arange(rows * top), side="right").astype(jnp.int32)
    grid = members.reshape(top, rows).T
    grid = grid[jax.random.permutation(jax.random.fold_in(own, 1), rows)]
    offset_by = jax.random.randint(jax.random.fold_in(own, 2), (rows, 1), 0, top)
    return jnp.take_along_axis(grid, (jnp.arange(top)[None, :] + offset_by) % top, axis=1)


def shares(amount, total, limit, lean, full):
    weights = [(1 << 20) // math.isqrt(grade ** lean) + 1 for grade in range(1, amount + 1)]
    largest = limit if full else min(limit, max(-(-total // amount), total * weights[0] // sum(weights)))
    least = 1 if total - largest >= amount - 1 else 0
    counts, spare = [largest] + [least] * (amount - 1), total - largest - least * (amount - 1)
    while spare > 0:
        movable = [i for i in range(1, amount) if counts[i] < largest] or [i for i in range(1, amount) if counts[i] < limit]
        whole, left = sum([weights[i] for i in movable]), spare
        for i in movable:
            more = min(limit - counts[i], max(1, left * weights[i] // whole), spare)
            counts[i] = counts[i] + more
            spare = spare - more
    return np.array(counts)


def centred(key, dims, width, reach, split=(), kind=jnp.bfloat16):
    array = jax.random.normal(key, dims, jnp.float32) * width
    if len(split) > 0:
        array = block_scale(key, dims, split, -0.22, 0.18) * array
    return jnp.clip(array, min=-reach, max=reach).astype(kind)


def setup_inputs(seed: int = 0) -> dict:
    splits = jax.random.split(jax.random.key(seed), 13)
    probe_field = centred(splits[0], (NODES, NT * PROBES), 1.0, 5.0, ((0, 4), (1, 8)))
    kappa = jnp.clip(jnp.exp(math.log(1.0) - 2.3025851 * jax.random.uniform(splits[1], (NODES,), jnp.float32) ** block_scale(splits[1], (NODES,), ((0, 4),), -0.2, 0.2)), 0.1, 1.0)
    theta_space = jnp.clip(jnp.exp(math.log(1.0) - 1.2039728 * jax.random.uniform(splits[2], (NT,), jnp.float32) ** block_scale(splits[2], (NT,), ((0, 8),), -0.2, 0.2)), 0.3, 1.0)
    theta_time = jnp.clip(jnp.exp(math.log(0.8) - 1.3862944 * jax.random.uniform(splits[3], (NT,), jnp.float32) ** block_scale(splits[3], (NT,), ((0, 8),), -0.2, 0.2)), 0.2, 0.8)
    diag_blocks = draw_diag_blocks(jax.random.fold_in(splits[12], 71), 0)
    off_blocks = centred(splits[5], (NB, NNZ_OFF, BLOCK, BLOCK), (0.8 / (BLOCK * NNZ_OFF) ** 0.5), 0.375, ((0, 4),))
    block_cols = plant(jax.random.randint(splits[6], (NB, NNZ_OFF), 0, NB_DEV + 2 * HALO_B), jax.random.fold_in(splits[6], 1), 0, (NB_DEV + 2 * HALO_B) - 1).astype(jnp.int32)
    halo_needs = plant(jax.random.randint(splits[7], (NEEDS,), 0, NB_DEV), jax.random.fold_in(splits[7], 1), 0, NB_DEV - 1).astype(jnp.int32)
    covariates = centred(splits[8], (OBS, NCOV), 0.7, 4.0, ((0, 32),))
    obs_owner_keys = jax.random.split(jax.random.fold_in(splits[9], 1), OBS // OBS_DEV)
    obs_owner_turns = jax.random.permutation(jax.random.fold_in(splits[9], 3), OBS // OBS_DEV)
    obs_owner = jax.vmap(lambda own, number: routed_block(jax.random.fold_in(splits[9], 2), own, number, OBS_DEV, N_SPACE, 1, CAP, 1))(obs_owner_keys, obs_owner_turns).reshape((OBS, 1))
    obs_cell = plant(jax.random.randint(splits[10], (OBS,), 0, NODES_DEV * T_DEV), jax.random.fold_in(splits[10], 1), 0, (NODES_DEV * T_DEV) - 1).astype(jnp.int32)
    svc_coef = centred(splits[11], (NODES, NCOV), NCOV ** -0.5, 0.375, ((0, 4),))
    return {"probe_field": probe_field, "kappa": kappa, "theta_space": theta_space, "theta_time": theta_time, "diag_blocks": diag_blocks, "off_blocks": off_blocks, "block_cols": block_cols, "halo_needs": halo_needs, "covariates": covariates, "obs_owner": obs_owner, "obs_cell": obs_cell, "svc_coef": svc_coef}


relaxation = 0.6


def reference(probe_field, kappa, theta_space, theta_time, diag_blocks, off_blocks, block_cols, halo_needs, covariates, obs_owner, obs_cell, svc_coef):
    columns = NT * PROBES
    width_local = NB_DEV + 2 * HALO_B
    probe_vals = probe_field.astype(jnp.float32)
    sdiag = jnp.diagonal(diag_blocks.astype(jnp.float32), axis1=1, axis2=2).reshape(NODES)
    scale_space = jnp.repeat(theta_space, PROBES)[None, :]
    scale_time = jnp.repeat(theta_time, PROBES)[None, :]
    base_diag = scale_space * sdiag[:, None] + 2.0 * scale_time + kappa[:, None]

    row_ids = jnp.arange(OBS, dtype=jnp.int32)
    slab = (row_ids // OBS_DEV) % N_TM
    owner = obs_owner[:, 0]
    node_ids = owner * NODES_DEV + obs_cell // T_DEV
    time_ids = slab * T_DEV + obs_cell % T_DEV
    eta = jnp.sum(covariates.astype(jnp.float32) * svc_coef[node_ids].astype(jnp.float32), axis=1)
    obs_weight = jnp.exp(eta)
    counted = jax.ops.segment_sum(obs_weight, node_ids * NT + time_ids, num_segments=NODES * NT)
    obs_diag = jnp.repeat(counted.reshape(NODES, NT), PROBES, axis=1)
    full_diag = base_diag + obs_diag

    block_ids = jnp.arange(NB, dtype=jnp.int32)
    space_of = block_ids // NB_DEV
    needs = halo_needs.reshape(N_SPACE, 2, HALO_B)

    def global_column(local):
        own = space_of * NB_DEV + local
        low_slot = jnp.clip(local - NB_DEV, 0, HALO_B - 1)
        low_block = needs[space_of, 0, low_slot]
        low_global = jnp.where(space_of > 0, (space_of - 1) * NB_DEV + low_block, NB)
        high_slot = jnp.clip(local - NB_DEV - HALO_B, 0, HALO_B - 1)
        high_block = needs[space_of, 1, high_slot]
        high_global = jnp.where(space_of < N_SPACE - 1, (space_of + 1) * NB_DEV + high_block, NB)
        return jnp.where(local < NB_DEV, own, jnp.where(local < NB_DEV + HALO_B, low_global, high_global)).astype(jnp.int32)

    local_ids = jnp.arange(width_local, dtype=jnp.int32)
    picks = (block_cols[:, :, None] == local_ids[None, None, :]).astype(jnp.float32)
    own_pick = ((block_ids - space_of * NB_DEV)[:, None] == local_ids[None, :]).astype(jnp.float32)
    combined = jnp.einsum('bkm,bkij->bmij', picks, off_blocks.astype(jnp.float32))
    combined = combined + own_pick[:, :, None, None] * diag_blocks.astype(jnp.float32)[:, None, :, :]
    combined = lax.optimization_barrier(combined.astype(jnp.bfloat16)).astype(jnp.float32)
    global_cols = [global_column(jnp.full((NB,), index, jnp.int32)) for index in range(width_local)]

    def spatial(field):
        blocks = field.reshape(NB, BLOCK, columns)
        padded = jnp.concatenate([blocks, jnp.zeros((1, BLOCK, columns), field.dtype)], axis=0)
        total = jnp.zeros((NB, BLOCK, columns), jnp.float32)
        for index in range(width_local):
            picked = padded[global_cols[index]]
            total = total + jnp.einsum('bij,bjc->bic', combined[:, index], picked.astype(jnp.float32))
        return total.reshape(NODES, columns)

    def temporal(field):
        values = field.astype(jnp.float32).reshape(NODES, NT, PROBES)
        padded = jnp.pad(values, ((0, 0), (1, 1), (0, 0)))
        return (2.0 * values - padded[:, :-2] - padded[:, 2:]).reshape(NODES, columns)

    solution = relaxation * probe_vals / base_diag
    for sweep in range(ITERS):
        rounded = lax.optimization_barrier(solution.astype(jnp.bfloat16))
        applied = scale_space * spatial(rounded) + scale_time * temporal(rounded) + (kappa[:, None] + obs_diag) * rounded.astype(jnp.float32)
        solution = solution + relaxation * (probe_vals - applied) / full_diag
    rounded = solution.astype(jnp.bfloat16)
    grad_space = jnp.sum(probe_vals * spatial(rounded), axis=0) / NODES
    grad_time = jnp.sum(probe_vals * temporal(rounded), axis=0) / NODES
    return solution, jnp.stack([grad_space, grad_time])
```

```python
import jax
import jax.numpy as jnp
from jax import lax
from jax.sharding import PartitionSpec as P

NB_DEV = 8
BLOCK = 128
HALO_B = 2
T_DEV = 4
PROBES = 64
NCOV = 256
OBS_DEV = 2048
ITERS = 4
NODES_DEV = 1024


relaxation = 0.6


def with_halo(array, sides, width):
    for axis, dim in sides:
        peers, length = (lax.axis_size(axis), array.shape[dim])
        up = [(i, (i + 1) % peers) for i in range(peers - 1)]
        down = [(j, i) for i, j in up]
        last = lax.slice_in_dim(array, length - width, length, axis=dim)
        initial = lax.slice_in_dim(array, 0, width, axis=dim)
        before = lax.ppermute(last, axis, up)
        after = lax.ppermute(initial, axis, down)
        array = jnp.concatenate([before, array, after], axis=dim)
    return array


def shards(
    probe_field,
    kappa,
    theta_space,
    theta_time,
    diag_blocks,
    off_blocks,
    block_cols,
    halo_needs,
    covariates,
    obs_owner,
    obs_cell,
    svc_coef,
):
    space_count = lax.axis_size("space")
    columns = probe_field.shape[1]
    width_local = NB_DEV + 2 * HALO_B
    probe_vals = probe_field.astype(jnp.float32)
    sdiag = jnp.diagonal(diag_blocks, axis1=1, axis2=2).astype(jnp.float32).reshape(NODES_DEV)
    scale_space = jnp.repeat(theta_space, PROBES)[None, :]
    scale_time = jnp.repeat(theta_time, PROBES)[None, :]
    base_diag = scale_space * sdiag[:, None] + 2.0 * scale_time + kappa[:, None]
    local_ids = jnp.arange(width_local, dtype=jnp.int32)
    picks = (block_cols[:, :, None] == local_ids[None, None, :]).astype(jnp.float32)
    own_pick = (jnp.arange(NB_DEV, dtype=jnp.int32)[:, None] == local_ids[None, :]).astype(
        jnp.float32
    )
    combined = jnp.einsum("bkm,bkij->bimj", picks, off_blocks.astype(jnp.float32))
    combined = combined + jnp.einsum("bm,bij->bimj", own_pick, diag_blocks.astype(jnp.float32))
    combined = combined.astype(jnp.bfloat16).reshape(NODES_DEV, width_local * BLOCK)
    own_part = combined[:, :NODES_DEV]
    lower_part = combined[:, NODES_DEV : NODES_DEV + HALO_B * BLOCK]
    upper_part = combined[:, NODES_DEV + HALO_B * BLOCK :]

    space_index = lax.axis_index("space")
    up = [(i, i + 1) for i in range(space_count - 1)]
    down = [(i + 1, i) for i in range(space_count - 1)]
    upper_wants = lax.ppermute(halo_needs[:HALO_B], "space", down)
    lower_wants = lax.ppermute(halo_needs[HALO_B:], "space", up)

    def pick_blocks(blocks, wanted):
        return jnp.concatenate(
            [lax.dynamic_index_in_dim(blocks, wanted[j], axis=0, keepdims=False) for j in range(HALO_B)],
            axis=0,
        )

    def spatial(field):
        blocks = field.reshape(NB_DEV, BLOCK, columns)
        lower = lax.ppermute(pick_blocks(blocks, upper_wants), "space", up)
        upper = lax.ppermute(pick_blocks(blocks, lower_wants), "space", down)
        total = jnp.dot(own_part, field, preferred_element_type=jnp.float32)
        total = total + jnp.dot(lower_part, lower, preferred_element_type=jnp.float32)
        total = total + jnp.dot(upper_part, upper, preferred_element_type=jnp.float32)
        return total

    def temporal(field):
        arrived = with_halo(field, (("tm", 1),), PROBES)
        return (
            2.0 * field.astype(jnp.float32)
            - arrived[:, :columns].astype(jnp.float32)
            - arrived[:, 2 * PROBES :].astype(jnp.float32)
        )

    solution = relaxation * probe_vals / base_diag
    rounded = lax.optimization_barrier(solution.astype(jnp.bfloat16))
    first_space = spatial(rounded)
    first_time = temporal(rounded)
    nodes_dev = svc_coef.shape[0]
    svc_all = lax.all_gather(svc_coef, "space", axis=0, tiled=True)
    owner = obs_owner[:, 0]
    coef_rows = svc_all[owner * nodes_dev + obs_cell // T_DEV]
    eta = jnp.einsum("rc,rc->r", covariates, coef_rows, preferred_element_type=jnp.float32)
    obs_weight = jnp.exp(eta)
    bins = owner * (nodes_dev * T_DEV) + obs_cell
    local_counts = jax.ops.segment_sum(
        obs_weight, bins, num_segments=space_count * nodes_dev * T_DEV
    )
    counted = lax.psum_scatter(local_counts, "space", scatter_dimension=0, tiled=True)
    obs_diag = jnp.repeat(counted.reshape(NODES_DEV, T_DEV), PROBES, axis=1)
    full_diag = base_diag + obs_diag
    local_diag = kappa[:, None] + obs_diag
    applied = (
        scale_space * first_space
        + scale_time * first_time
        + local_diag * rounded.astype(jnp.float32)
    )
    solution = solution + relaxation * (probe_vals - applied) / full_diag
    for sweep in range(ITERS - 1):
        rounded = lax.optimization_barrier(solution.astype(jnp.bfloat16))
        applied = (
            scale_space * spatial(rounded)
            + scale_time * temporal(rounded)
            + local_diag * rounded.astype(jnp.float32)
        )
        solution = solution + relaxation * (probe_vals - applied) / full_diag
    rounded = solution.astype(jnp.bfloat16)
    partial_sums = jnp.stack(
        [
            jnp.sum(probe_vals * spatial(rounded), axis=0),
            jnp.sum(probe_vals * temporal(rounded), axis=0),
        ]
    )
    totals = lax.psum(partial_sums, "space")
    grads = totals / (NODES_DEV * space_count)
    return (solution, grads)


def solution(mesh):
    return jax.shard_map(
        shards,
        mesh=mesh,
        in_specs=(
            P("space", "tm"),
            P("space"),
            P("tm"),
            P("tm"),
            P("space", None, None),
            P("space", None, None, None),
            P("space", None),
            P("space"),
            P(("space", "tm"), None),
            P(("space", "tm"), None),
            P(("space", "tm")),
            P("space", None),
        ),
        out_specs=(P("space", "tm"), P(None, "tm")),
        check_vma=False,
    )
```

```python
import jax
import jax.numpy as jnp
from jax import lax
from jax.sharding import PartitionSpec as P

NB_DEV = 8
BLOCK = 128
HALO_B = 2
T_DEV = 4
PROBES = 64
NCOV = 256
OBS_DEV = 2048
ITERS = 4
NODES_DEV = 1024


relaxation = 0.6


def with_halo(array, sides, width):
    for axis, dim in sides:
        peers, length = (lax.axis_size(axis), array.shape[dim])
        up = [(i, (i + 1) % peers) for i in range(peers - 1)]
        down = [(j, i) for i, j in up]
        last = lax.slice_in_dim(array, length - width, length, axis=dim)
        initial = lax.slice_in_dim(array, 0, width, axis=dim)
        before = lax.ppermute(last, axis, up)
        after = lax.ppermute(initial, axis, down)
        array = jnp.concatenate([before, array, after], axis=dim)
    return array


def shards(
    probe_field,
    kappa,
    theta_space,
    theta_time,
    diag_blocks,
    off_blocks,
    block_cols,
    halo_needs,
    covariates,
    obs_owner,
    obs_cell,
    svc_coef,
):
    space_count = lax.axis_size("space")
    columns = probe_field.shape[1]
    width_local = NB_DEV + 2 * HALO_B
    probe_vals = probe_field.astype(jnp.float32)
    sdiag = jnp.diagonal(diag_blocks, axis1=1, axis2=2).astype(jnp.float32).reshape(NODES_DEV)
    scale_space = jnp.repeat(theta_space, PROBES)[None, :]
    scale_time = jnp.repeat(theta_time, PROBES)[None, :]
    base_diag = scale_space * sdiag[:, None] + 2.0 * scale_time + kappa[:, None]
    local_ids = jnp.arange(width_local, dtype=jnp.int32)
    picks = (block_cols[:, :, None] == local_ids[None, None, :]).astype(jnp.float32)
    own_pick = (jnp.arange(NB_DEV, dtype=jnp.int32)[:, None] == local_ids[None, :]).astype(
        jnp.float32
    )
    combined = jnp.einsum("bkm,bkij->bimj", picks, off_blocks.astype(jnp.float32))
    combined = combined + jnp.einsum("bm,bij->bimj", own_pick, diag_blocks.astype(jnp.float32))
    combined = combined.astype(jnp.bfloat16).reshape(NODES_DEV, width_local * BLOCK)
    own_part = combined[:, :NODES_DEV]
    lower_part = combined[:, NODES_DEV : NODES_DEV + HALO_B * BLOCK]
    upper_part = combined[:, NODES_DEV + HALO_B * BLOCK :]

    space_index = lax.axis_index("space")
    up = [(i, i + 1) for i in range(space_count - 1)]
    down = [(i + 1, i) for i in range(space_count - 1)]
    upper_wants = lax.ppermute(halo_needs[:HALO_B], "space", down)
    lower_wants = lax.ppermute(halo_needs[HALO_B:], "space", up)

    def pick_blocks(blocks, wanted):
        return jnp.concatenate(
            [lax.dynamic_index_in_dim(blocks, wanted[j], axis=0, keepdims=False) for j in range(HALO_B)],
            axis=0,
        )

    def spatial(field):
        blocks = field.reshape(NB_DEV, BLOCK, columns)
        lower = lax.ppermute(pick_blocks(blocks, upper_wants), "space", up)
        upper = lax.ppermute(pick_blocks(blocks, lower_wants), "space", down)
        total = jnp.dot(own_part, field, preferred_element_type=jnp.float32)
        total = total + jnp.dot(lower_part, lower, preferred_element_type=jnp.float32)
        total = total + jnp.dot(upper_part, upper, preferred_element_type=jnp.float32)
        return total

    def temporal(field):
        arrived = with_halo(field, (("tm", 1),), PROBES)
        return (
            2.0 * field.astype(jnp.float32)
            - arrived[:, :columns].astype(jnp.float32)
            - arrived[:, 2 * PROBES :].astype(jnp.float32)
        )

    solution = relaxation * probe_vals / base_diag
    rounded = lax.optimization_barrier(solution.astype(jnp.bfloat16))
    first_space = spatial(rounded)
    first_time = temporal(rounded)
    nodes_dev = svc_coef.shape[0]
    svc_all = lax.all_gather(svc_coef, "space", axis=0, tiled=True)
    owner = obs_owner[:, 0]
    coef_rows = svc_all[owner * nodes_dev + obs_cell // T_DEV]
    eta = jnp.einsum("rc,rc->r", covariates, coef_rows, preferred_element_type=jnp.float32)
    obs_weight = jnp.exp(eta)
    bins = owner * (nodes_dev * T_DEV) + obs_cell
    local_counts = jax.ops.segment_sum(
        obs_weight, bins, num_segments=space_count * nodes_dev * T_DEV
    ).reshape(space_count, nodes_dev * T_DEV)
    counted = jnp.sum(
        lax.all_to_all(local_counts, "space", split_axis=0, concat_axis=0, tiled=True), axis=0
    )
    obs_diag = jnp.repeat(counted.reshape(NODES_DEV, T_DEV), PROBES, axis=1)
    full_diag = base_diag + obs_diag
    local_diag = kappa[:, None] + obs_diag
    applied = (
        scale_space * first_space
        + scale_time * first_time
        + local_diag * rounded.astype(jnp.float32)
    )
    solution = solution + relaxation * (probe_vals - applied) / full_diag
    for sweep in range(ITERS - 1):
        rounded = lax.optimization_barrier(solution.astype(jnp.bfloat16))
        applied = (
            scale_space * spatial(rounded)
            + scale_time * temporal(rounded)
            + local_diag * rounded.astype(jnp.float32)
        )
        solution = solution + relaxation * (probe_vals - applied) / full_diag
    rounded = solution.astype(jnp.bfloat16)
    partial_sums = jnp.stack(
        [
            jnp.sum(probe_vals * spatial(rounded), axis=0),
            jnp.sum(probe_vals * temporal(rounded), axis=0),
        ]
    )
    totals = lax.psum(partial_sums, "space")
    grads = totals / (NODES_DEV * space_count)
    return (solution, grads)


def solution(mesh):
    return jax.shard_map(
        shards,
        mesh=mesh,
        in_specs=(
            P("space", "tm"),
            P("space"),
            P("tm"),
            P("tm"),
            P("space", None, None),
            P("space", None, None, None),
            P("space", None),
            P("space"),
            P(("space", "tm"), None),
            P(("space", "tm"), None),
            P(("space", "tm")),
            P("space", None),
        ),
        out_specs=(P("space", "tm"), P(None, "tm")),
        check_vma=False,
    )
```

```python
import jax
import jax.numpy as jnp
from jax import lax
from jax.sharding import PartitionSpec as P

NB_DEV = 8
BLOCK = 128
HALO_B = 2
T_DEV = 4
PROBES = 64
NCOV = 256
OBS_DEV = 2048
ITERS = 4
NODES_DEV = 1024


relaxation = 0.6


def with_halo(array, sides, width):
    for axis, dim in sides:
        peers, length = (lax.axis_size(axis), array.shape[dim])
        up = [(i, (i + 1) % peers) for i in range(peers - 1)]
        down = [(j, i) for i, j in up]
        last = lax.slice_in_dim(array, length - width, length, axis=dim)
        initial = lax.slice_in_dim(array, 0, width, axis=dim)
        before = lax.ppermute(last, axis, up)
        after = lax.ppermute(initial, axis, down)
        array = jnp.concatenate([before, array, after], axis=dim)
    return array


def shards(
    probe_field,
    kappa,
    theta_space,
    theta_time,
    diag_blocks,
    off_blocks,
    block_cols,
    halo_needs,
    covariates,
    obs_owner,
    obs_cell,
    svc_coef,
):
    space_count = lax.axis_size("space")
    columns = probe_field.shape[1]
    width_local = NB_DEV + 2 * HALO_B
    probe_vals = probe_field.astype(jnp.float32)
    eye = jnp.arange(BLOCK)[:, None] == jnp.arange(BLOCK)[None, :]
    sdiag = jnp.sum(
        jnp.where(eye[None], diag_blocks.astype(jnp.float32), 0.0), axis=2
    ).reshape(NODES_DEV)
    scale_space = jnp.repeat(theta_space, PROBES)[None, :]
    scale_time = jnp.repeat(theta_time, PROBES)[None, :]
    base_diag = scale_space * sdiag[:, None] + 2.0 * scale_time + kappa[:, None]
    local_ids = jnp.arange(width_local, dtype=jnp.int32)
    picks = block_cols[:, None, None, :] == local_ids[None, None, :, None]
    off_f32 = off_blocks.astype(jnp.float32).transpose(0, 2, 1, 3)
    combined = jnp.sum(
        jnp.where(picks[..., None], off_f32[:, :, None, :, :], 0.0), axis=3
    )
    own_pick = jnp.arange(NB_DEV, dtype=jnp.int32)[:, None] == local_ids[None, :]
    combined = combined + jnp.where(
        own_pick[:, None, :, None], diag_blocks.astype(jnp.float32)[:, :, None, :], 0.0
    )
    combined = combined.astype(jnp.bfloat16).reshape(NODES_DEV, width_local * BLOCK)
    own_part = combined[:, :NODES_DEV]
    lower_part = combined[:, NODES_DEV : NODES_DEV + HALO_B * BLOCK]
    upper_part = combined[:, NODES_DEV + HALO_B * BLOCK :]

    space_index = lax.axis_index("space")
    up = [(i, i + 1) for i in range(space_count - 1)]
    down = [(i + 1, i) for i in range(space_count - 1)]
    upper_wants = lax.ppermute(halo_needs[:HALO_B], "space", down)
    lower_wants = lax.ppermute(halo_needs[HALO_B:], "space", up)

    def pick_blocks(blocks, wanted):
        return jnp.concatenate(
            [lax.dynamic_index_in_dim(blocks, wanted[j], axis=0, keepdims=False) for j in range(HALO_B)],
            axis=0,
        )

    def spatial(field):
        blocks = field.reshape(NB_DEV, BLOCK, columns)
        lower = lax.ppermute(pick_blocks(blocks, upper_wants), "space", up)
        upper = lax.ppermute(pick_blocks(blocks, lower_wants), "space", down)
        total = jnp.dot(own_part, field, preferred_element_type=jnp.float32)
        total = total + jnp.dot(lower_part, lower, preferred_element_type=jnp.float32)
        total = total + jnp.dot(upper_part, upper, preferred_element_type=jnp.float32)
        return total

    def temporal(field):
        arrived = with_halo(field, (("tm", 1),), PROBES)
        return (
            2.0 * field.astype(jnp.float32)
            - arrived[:, :columns].astype(jnp.float32)
            - arrived[:, 2 * PROBES :].astype(jnp.float32)
        )

    solution = relaxation * probe_vals / base_diag
    rounded = lax.optimization_barrier(solution.astype(jnp.bfloat16))
    first_space = spatial(rounded)
    first_time = temporal(rounded)
    nodes_dev = svc_coef.shape[0]
    svc_all = lax.all_gather(svc_coef, "space", axis=0, tiled=True)
    owner = obs_owner[:, 0]
    coef_rows = svc_all[owner * nodes_dev + obs_cell // T_DEV]
    eta = jnp.einsum("rc,rc->r", covariates, coef_rows, preferred_element_type=jnp.float32)
    obs_weight = jnp.exp(eta)
    bins = owner * (nodes_dev * T_DEV) + obs_cell
    local_counts = jax.ops.segment_sum(
        obs_weight, bins, num_segments=space_count * nodes_dev * T_DEV
    ).reshape(space_count, nodes_dev * T_DEV)
    counted = jnp.sum(
        lax.all_to_all(local_counts, "space", split_axis=0, concat_axis=0, tiled=True), axis=0
    )
    obs_diag = jnp.repeat(counted.reshape(NODES_DEV, T_DEV), PROBES, axis=1)
    full_diag = base_diag + obs_diag
    local_diag = kappa[:, None] + obs_diag
    applied = (
        scale_space * first_space
        + scale_time * first_time
        + local_diag * rounded.astype(jnp.float32)
    )
    solution = solution + relaxation * (probe_vals - applied) / full_diag
    for sweep in range(ITERS - 1):
        rounded = lax.optimization_barrier(solution.astype(jnp.bfloat16))
        applied = (
            scale_space * spatial(rounded)
            + scale_time * temporal(rounded)
            + local_diag * rounded.astype(jnp.float32)
        )
        solution = solution + relaxation * (probe_vals - applied) / full_diag
    rounded = solution.astype(jnp.bfloat16)
    partial_sums = jnp.stack(
        [
            jnp.sum(probe_vals * spatial(rounded), axis=0),
            jnp.sum(probe_vals * temporal(rounded), axis=0),
        ]
    )
    totals = lax.psum(partial_sums, "space")
    grads = totals / (NODES_DEV * space_count)
    return (solution, grads)


def solution(mesh):
    return jax.shard_map(
        shards,
        mesh=mesh,
        in_specs=(
            P("space", "tm"),
            P("space"),
            P("tm"),
            P("tm"),
            P("space", None, None),
            P("space", None, None, None),
            P("space", None),
            P("space"),
            P(("space", "tm"), None),
            P(("space", "tm"), None),
            P(("space", "tm")),
            P("space", None),
        ),
        out_specs=(P("space", "tm"), P(None, "tm")),
        check_vma=False,
    )
```

```python
import jax
import jax.numpy as jnp
from jax import lax
from jax.sharding import PartitionSpec as P

NB_DEV = 8
BLOCK = 128
HALO_B = 2
T_DEV = 4
PROBES = 64
NCOV = 256
OBS_DEV = 2048
ITERS = 4
NODES_DEV = 1024


relaxation = 0.6


def with_halo(array, sides, width):
    for axis, dim in sides:
        peers, length = (lax.axis_size(axis), array.shape[dim])
        up = [(i, (i + 1) % peers) for i in range(peers - 1)]
        down = [(j, i) for i, j in up]
        last = lax.slice_in_dim(array, length - width, length, axis=dim)
        initial = lax.slice_in_dim(array, 0, width, axis=dim)
        before = lax.ppermute(last, axis, up)
        after = lax.ppermute(initial, axis, down)
        array = jnp.concatenate([before, array, after], axis=dim)
    return array


def shards(
    probe_field,
    kappa,
    theta_space,
    theta_time,
    diag_blocks,
    off_blocks,
    block_cols,
    halo_needs,
    covariates,
    obs_owner,
    obs_cell,
    svc_coef,
):
    space_count = lax.axis_size("space")
    columns = probe_field.shape[1]
    width_local = NB_DEV + 2 * HALO_B
    probe_vals = probe_field.astype(jnp.float32)
    sdiag = jnp.diagonal(diag_blocks, axis1=1, axis2=2).astype(jnp.float32).reshape(NODES_DEV)
    scale_space = jnp.repeat(theta_space, PROBES)[None, :]
    scale_time = jnp.repeat(theta_time, PROBES)[None, :]
    base_diag = scale_space * sdiag[:, None] + 2.0 * scale_time + kappa[:, None]
    local_ids = jnp.arange(width_local, dtype=jnp.int32)
    picks = (block_cols[:, :, None] == local_ids[None, None, :]).astype(jnp.float32)
    own_pick = (jnp.arange(NB_DEV, dtype=jnp.int32)[:, None] == local_ids[None, :]).astype(
        jnp.float32
    )
    combined = jnp.einsum("bkm,bkij->bimj", picks, off_blocks.astype(jnp.float32))
    combined = combined + jnp.einsum("bm,bij->bimj", own_pick, diag_blocks.astype(jnp.float32))
    combined = combined.astype(jnp.bfloat16).reshape(NODES_DEV, width_local * BLOCK)
    own_part = combined[:, :NODES_DEV]
    lower_part = combined[:, NODES_DEV : NODES_DEV + HALO_B * BLOCK]
    upper_part = combined[:, NODES_DEV + HALO_B * BLOCK :]

    space_index = lax.axis_index("space")
    up = [(i, i + 1) for i in range(space_count - 1)]
    down = [(i + 1, i) for i in range(space_count - 1)]
    upper_wants = lax.ppermute(halo_needs[:HALO_B], "space", down)
    lower_wants = lax.ppermute(halo_needs[HALO_B:], "space", up)

    def pick_blocks(blocks, wanted):
        return jnp.concatenate(
            [lax.dynamic_index_in_dim(blocks, wanted[j], axis=0, keepdims=False) for j in range(HALO_B)],
            axis=0,
        )

    def spatial(field):
        blocks = field.reshape(NB_DEV, BLOCK, columns)
        lower = lax.ppermute(pick_blocks(blocks, upper_wants), "space", up)
        upper = lax.ppermute(pick_blocks(blocks, lower_wants), "space", down)
        total = jnp.dot(own_part, field, preferred_element_type=jnp.float32)
        total = total + jnp.dot(lower_part, lower, preferred_element_type=jnp.float32)
        total = total + jnp.dot(upper_part, upper, preferred_element_type=jnp.float32)
        return total

    def temporal(field):
        arrived = with_halo(field, (("tm", 1),), PROBES)
        return (
            2.0 * field.astype(jnp.float32)
            - arrived[:, :columns].astype(jnp.float32)
            - arrived[:, 2 * PROBES :].astype(jnp.float32)
        )

    solution = relaxation * probe_vals / base_diag
    rounded = lax.optimization_barrier(solution.astype(jnp.bfloat16))
    first_space = spatial(rounded)
    first_time = temporal(rounded)
    nodes_dev = svc_coef.shape[0]
    tables = [svc_coef] + [
        lax.ppermute(svc_coef, "space", [(i, (i + k) % space_count) for i in range(space_count)])
        for k in range(1, space_count)
    ]
    svc_all = jnp.concatenate(tables, axis=0)
    owner = obs_owner[:, 0]
    shift = (lax.axis_index("space") - owner) % space_count
    coef_rows = svc_all[shift * nodes_dev + obs_cell // T_DEV]
    eta = jnp.einsum("rc,rc->r", covariates, coef_rows, preferred_element_type=jnp.float32)
    obs_weight = jnp.exp(eta)
    bins = owner * (nodes_dev * T_DEV) + obs_cell
    local_counts = jax.ops.segment_sum(
        obs_weight, bins, num_segments=space_count * nodes_dev * T_DEV
    ).reshape(space_count, nodes_dev * T_DEV)
    counted = jnp.sum(
        lax.all_to_all(local_counts, "space", split_axis=0, concat_axis=0, tiled=True), axis=0
    )
    obs_diag = jnp.repeat(counted.reshape(NODES_DEV, T_DEV), PROBES, axis=1)
    full_diag = base_diag + obs_diag
    local_diag = kappa[:, None] + obs_diag
    applied = (
        scale_space * first_space
        + scale_time * first_time
        + local_diag * rounded.astype(jnp.float32)
    )
    solution = solution + relaxation * (probe_vals - applied) / full_diag
    for sweep in range(ITERS - 1):
        rounded = lax.optimization_barrier(solution.astype(jnp.bfloat16))
        applied = (
            scale_space * spatial(rounded)
            + scale_time * temporal(rounded)
            + local_diag * rounded.astype(jnp.float32)
        )
        solution = solution + relaxation * (probe_vals - applied) / full_diag
    rounded = solution.astype(jnp.bfloat16)
    partial_sums = jnp.stack(
        [
            jnp.sum(probe_vals * spatial(rounded), axis=0),
            jnp.sum(probe_vals * temporal(rounded), axis=0),
        ]
    )
    totals = lax.psum(partial_sums, "space")
    grads = totals / (NODES_DEV * space_count)
    return (solution, grads)


def solution(mesh):
    return jax.shard_map(
        shards,
        mesh=mesh,
        in_specs=(
            P("space", "tm"),
            P("space"),
            P("tm"),
            P("tm"),
            P("space", None, None),
            P("space", None, None, None),
            P("space", None),
            P("space"),
            P(("space", "tm"), None),
            P(("space", "tm"), None),
            P(("space", "tm")),
            P("space", None),
        ),
        out_specs=(P("space", "tm"), P(None, "tm")),
        check_vma=False,
    )
```

```python
import jax
import jax.numpy as jnp
from jax import lax
from jax.sharding import PartitionSpec as P

NB_DEV = 8
BLOCK = 128
HALO_B = 2
T_DEV = 4
PROBES = 64
NCOV = 256
OBS_DEV = 2048
ITERS = 4
NODES_DEV = 1024


relaxation = 0.6


def with_halo(array, sides, width):
    for axis, dim in sides:
        peers, length = (lax.axis_size(axis), array.shape[dim])
        up = [(i, (i + 1) % peers) for i in range(peers - 1)]
        down = [(j, i) for i, j in up]
        last = lax.slice_in_dim(array, length - width, length, axis=dim)
        initial = lax.slice_in_dim(array, 0, width, axis=dim)
        before = lax.ppermute(last, axis, up)
        after = lax.ppermute(initial, axis, down)
        array = jnp.concatenate([before, array, after], axis=dim)
    return array


def shards(
    probe_field,
    kappa,
    theta_space,
    theta_time,
    diag_blocks,
    off_blocks,
    block_cols,
    halo_needs,
    covariates,
    obs_owner,
    obs_cell,
    svc_coef,
):
    space_count = lax.axis_size("space")
    columns = probe_field.shape[1]
    width_local = NB_DEV + 2 * HALO_B
    probe_vals = probe_field.astype(jnp.float32)
    eye = jnp.arange(BLOCK)[:, None] == jnp.arange(BLOCK)[None, :]
    sdiag = jnp.sum(jnp.where(eye[None], diag_blocks.astype(jnp.float32), 0.0), axis=2).reshape(
        NODES_DEV
    )
    scale_space = jnp.repeat(theta_space, PROBES)[None, :]
    scale_time = jnp.repeat(theta_time, PROBES)[None, :]
    base_diag = scale_space * sdiag[:, None] + 2.0 * scale_time + kappa[:, None]
    local_ids = jnp.arange(width_local, dtype=jnp.int32)
    picks = (block_cols[:, :, None] == local_ids[None, None, :]).astype(jnp.float32)
    own_pick = (jnp.arange(NB_DEV, dtype=jnp.int32)[:, None] == local_ids[None, :]).astype(
        jnp.float32
    )
    combined = jnp.einsum("bkm,bkij->bimj", picks, off_blocks.astype(jnp.float32))
    combined = combined + jnp.einsum("bm,bij->bimj", own_pick, diag_blocks.astype(jnp.float32))
    combined = combined.astype(jnp.bfloat16).reshape(NODES_DEV, width_local * BLOCK)
    own_part = combined[:, :NODES_DEV]
    lower_part = combined[:, NODES_DEV : NODES_DEV + HALO_B * BLOCK]
    upper_part = combined[:, NODES_DEV + HALO_B * BLOCK :]
    own_t, lower_t, upper_t = own_part.T, lower_part.T, upper_part.T

    space_index = lax.axis_index("space")
    up = [(i, i + 1) for i in range(space_count - 1)]
    down = [(i + 1, i) for i in range(space_count - 1)]
    upper_wants = lax.ppermute(halo_needs[:HALO_B], "space", down)
    lower_wants = lax.ppermute(halo_needs[HALO_B:], "space", up)

    def pick_blocks(field, wanted):
        return jnp.concatenate(
            [lax.dynamic_slice_in_dim(field, wanted[j] * BLOCK, BLOCK, axis=0) for j in range(HALO_B)],
            axis=0,
        )

    def spatial(field):
        lower = lax.ppermute(pick_blocks(field, upper_wants), "space", up)
        upper = lax.ppermute(pick_blocks(field, lower_wants), "space", down)
        total = jnp.dot(field.T, own_t, preferred_element_type=jnp.float32)
        total = total + jnp.dot(lower.T, lower_t, preferred_element_type=jnp.float32)
        total = total + jnp.dot(upper.T, upper_t, preferred_element_type=jnp.float32)
        return total.T

    def temporal(field):
        arrived = with_halo(field, (("tm", 1),), PROBES)
        return (
            2.0 * field.astype(jnp.float32)
            - arrived[:, :columns].astype(jnp.float32)
            - arrived[:, 2 * PROBES :].astype(jnp.float32)
        )

    solution = relaxation * probe_vals / base_diag
    rounded = lax.optimization_barrier(solution.astype(jnp.bfloat16))
    first_space = spatial(rounded)
    first_time = temporal(rounded)
    nodes_dev = svc_coef.shape[0]
    tables = [svc_coef] + [
        lax.ppermute(svc_coef, "space", [(i, (i + k) % space_count) for i in range(space_count)])
        for k in range(1, space_count)
    ]
    svc_all = jnp.concatenate(tables, axis=0)
    owner = obs_owner[:, 0]
    shift = (lax.axis_index("space") - owner) % space_count
    coef_rows = svc_all[shift * nodes_dev + obs_cell // T_DEV]
    eta = jnp.einsum("rc,rc->r", covariates, coef_rows, preferred_element_type=jnp.float32)
    obs_weight = jnp.exp(eta)
    bins = owner * (nodes_dev * T_DEV) + obs_cell
    local_counts = jax.ops.segment_sum(
        obs_weight, bins, num_segments=space_count * nodes_dev * T_DEV
    ).reshape(space_count, nodes_dev * T_DEV)
    counted = jnp.sum(
        lax.all_to_all(local_counts, "space", split_axis=0, concat_axis=0, tiled=True), axis=0
    )
    obs_diag = jnp.repeat(counted.reshape(NODES_DEV, T_DEV), PROBES, axis=1)
    full_diag = base_diag + obs_diag
    local_diag = kappa[:, None] + obs_diag
    applied = (
        scale_space * first_space
        + scale_time * first_time
        + local_diag * rounded.astype(jnp.float32)
    )
    solution = solution + relaxation * (probe_vals - applied) / full_diag
    for sweep in range(ITERS - 1):
        rounded = lax.optimization_barrier(solution.astype(jnp.bfloat16))
        applied = (
            scale_space * spatial(rounded)
            + scale_time * temporal(rounded)
            + local_diag * rounded.astype(jnp.float32)
        )
        solution = solution + relaxation * (probe_vals - applied) / full_diag
    rounded = solution.astype(jnp.bfloat16)
    partial_sums = jnp.stack(
        [
            jnp.sum(probe_vals * spatial(rounded), axis=0),
            jnp.sum(probe_vals * temporal(rounded), axis=0),
        ]
    )
    totals = lax.psum(partial_sums, "space")
    grads = totals / (NODES_DEV * space_count)
    return (solution, grads)


def solution(mesh):
    return jax.shard_map(
        shards,
        mesh=mesh,
        in_specs=(
            P("space", "tm"),
            P("space"),
            P("tm"),
            P("tm"),
            P("space", None, None),
            P("space", None, None, None),
            P("space", None),
            P("space"),
            P(("space", "tm"), None),
            P(("space", "tm"), None),
            P(("space", "tm")),
            P("space", None),
        ),
        out_specs=(P("space", "tm"), P(None, "tm")),
        check_vma=False,
    )
```

```python
import jax
import jax.numpy as jnp
from jax import lax
from jax.sharding import PartitionSpec as P

NB_DEV = 8
BLOCK = 128
HALO_B = 2
T_DEV = 4
PROBES = 64
NCOV = 256
OBS_DEV = 2048
ITERS = 4
NODES_DEV = 1024


relaxation = 0.6


def with_halo(array, sides, width):
    for axis, dim in sides:
        peers, length = (lax.axis_size(axis), array.shape[dim])
        up = [(i, (i + 1) % peers) for i in range(peers - 1)]
        down = [(j, i) for i, j in up]
        last = lax.slice_in_dim(array, length - width, length, axis=dim)
        initial = lax.slice_in_dim(array, 0, width, axis=dim)
        before = lax.ppermute(last, axis, up)
        after = lax.ppermute(initial, axis, down)
        array = jnp.concatenate([before, array, after], axis=dim)
    return array


def shards(
    probe_field,
    kappa,
    theta_space,
    theta_time,
    diag_blocks,
    off_blocks,
    block_cols,
    halo_needs,
    covariates,
    obs_owner,
    obs_cell,
    svc_coef,
):
    space_count = lax.axis_size("space")
    columns = probe_field.shape[1]
    width_local = NB_DEV + 2 * HALO_B
    probe_vals = probe_field.astype(jnp.float32)
    eye = jnp.arange(BLOCK)[:, None] == jnp.arange(BLOCK)[None, :]
    sdiag = jnp.sum(jnp.where(eye[None], diag_blocks.astype(jnp.float32), 0.0), axis=2).reshape(
        NODES_DEV
    )
    scale_space = jnp.repeat(theta_space, PROBES)[None, :]
    scale_time = jnp.repeat(theta_time, PROBES)[None, :]
    base_diag = scale_space * sdiag[:, None] + 2.0 * scale_time + kappa[:, None]
    local_ids = jnp.arange(width_local, dtype=jnp.int32)
    picks = (block_cols[:, :, None] == local_ids[None, None, :]).astype(jnp.float32)
    own_pick = (jnp.arange(NB_DEV, dtype=jnp.int32)[:, None] == local_ids[None, :]).astype(
        jnp.float32
    )
    combined = jnp.einsum("bkm,bkij->bimj", picks, off_blocks.astype(jnp.float32))
    combined = combined + jnp.einsum("bm,bij->bimj", own_pick, diag_blocks.astype(jnp.float32))
    combined = combined.astype(jnp.bfloat16).reshape(NODES_DEV, width_local * BLOCK)
    own_part = combined[:, :NODES_DEV]
    lower_part = combined[:, NODES_DEV : NODES_DEV + HALO_B * BLOCK]
    upper_part = combined[:, NODES_DEV + HALO_B * BLOCK :]
    own_t, lower_t, upper_t = own_part.T, lower_part.T, upper_part.T

    space_index = lax.axis_index("space")
    up = [(i, i + 1) for i in range(space_count - 1)]
    down = [(i + 1, i) for i in range(space_count - 1)]
    upper_wants = lax.ppermute(halo_needs[:HALO_B], "space", down)
    lower_wants = lax.ppermute(halo_needs[HALO_B:], "space", up)

    def pick_blocks(field, wanted):
        return jnp.concatenate(
            [lax.dynamic_slice_in_dim(field, wanted[j] * BLOCK, BLOCK, axis=0) for j in range(HALO_B)],
            axis=0,
        )

    def spatial(field):
        lower = lax.ppermute(pick_blocks(field, upper_wants), "space", up)
        upper = lax.ppermute(pick_blocks(field, lower_wants), "space", down)
        total = jnp.dot(field.T, own_t, preferred_element_type=jnp.float32)
        total = total + jnp.dot(lower.T, lower_t, preferred_element_type=jnp.float32)
        total = total + jnp.dot(upper.T, upper_t, preferred_element_type=jnp.float32)
        return total.T

    def temporal(field):
        arrived = with_halo(field, (("tm", 1),), PROBES)
        return (
            2.0 * field.astype(jnp.float32)
            - arrived[:, :columns].astype(jnp.float32)
            - arrived[:, 2 * PROBES :].astype(jnp.float32)
        )

    solution = relaxation * probe_vals / base_diag
    rounded = lax.optimization_barrier(solution.astype(jnp.bfloat16))
    first_space = spatial(rounded)
    first_time = temporal(rounded)
    nodes_dev = svc_coef.shape[0]
    tables = [svc_coef] + [
        lax.ppermute(svc_coef, "space", [(i, (i + k) % space_count) for i in range(space_count)])
        for k in range(1, space_count)
    ]
    shifts = (lax.axis_index("space") - jnp.arange(space_count)) % space_count
    svc_all = jnp.stack(tables)[shifts].reshape(space_count * nodes_dev, svc_coef.shape[1])
    owner = obs_owner[:, 0]
    node_ids = owner * nodes_dev + obs_cell // T_DEV
    onehot = (node_ids[:, None] == jnp.arange(space_count * nodes_dev)[None, :]).astype(jnp.bfloat16)
    coef_rows = jnp.dot(onehot, svc_all, preferred_element_type=jnp.float32)
    eta = jnp.sum(covariates.astype(jnp.float32) * coef_rows, axis=1)
    obs_weight = jnp.exp(eta)
    high = lax.reduce_precision(obs_weight, exponent_bits=8, mantissa_bits=7)
    rest = obs_weight - high
    middle = lax.reduce_precision(rest, exponent_bits=8, mantissa_bits=7)
    low = rest - middle
    in_step = obs_cell[:, None] % T_DEV == jnp.arange(T_DEV)[None, :]
    parts = jnp.concatenate(
        [jnp.where(in_step, piece[:, None], 0.0) for piece in (high, middle, low)], axis=1
    ).astype(jnp.bfloat16)
    sums = lax.dot_general(
        onehot, parts, (((0,), (0,)), ((), ())), preferred_element_type=jnp.float32
    )
    local_counts = (sums[:, :T_DEV] + sums[:, T_DEV : 2 * T_DEV] + sums[:, 2 * T_DEV :]).reshape(
        space_count, nodes_dev * T_DEV
    )
    counted = jnp.sum(
        lax.all_to_all(local_counts, "space", split_axis=0, concat_axis=0, tiled=True), axis=0
    )
    obs_diag = jnp.repeat(counted.reshape(NODES_DEV, T_DEV), PROBES, axis=1)
    full_diag = base_diag + obs_diag
    local_diag = kappa[:, None] + obs_diag
    applied = (
        scale_space * first_space
        + scale_time * first_time
        + local_diag * rounded.astype(jnp.float32)
    )
    solution = solution + relaxation * (probe_vals - applied) / full_diag
    for sweep in range(ITERS - 1):
        rounded = lax.optimization_barrier(solution.astype(jnp.bfloat16))
        applied = (
            scale_space * spatial(rounded)
            + scale_time * temporal(rounded)
            + local_diag * rounded.astype(jnp.float32)
        )
        solution = solution + relaxation * (probe_vals - applied) / full_diag
    rounded = solution.astype(jnp.bfloat16)
    partial_sums = jnp.stack(
        [
            jnp.sum(probe_vals * spatial(rounded), axis=0),
            jnp.sum(probe_vals * temporal(rounded), axis=0),
        ]
    )
    totals = lax.psum(partial_sums, "space")
    grads = totals / (NODES_DEV * space_count)
    return (solution, grads)


def solution(mesh):
    return jax.shard_map(
        shards,
        mesh=mesh,
        in_specs=(
            P("space", "tm"),
            P("space"),
            P("tm"),
            P("tm"),
            P("space", None, None),
            P("space", None, None, None),
            P("space", None),
            P("space"),
            P(("space", "tm"), None),
            P(("space", "tm"), None),
            P(("space", "tm")),
            P("space", None),
        ),
        out_specs=(P("space", "tm"), P(None, "tm")),
        check_vma=False,
    )
```

```python
import jax
import jax.numpy as jnp
from jax import lax
from jax.sharding import PartitionSpec as P

NB_DEV = 8
BLOCK = 128
HALO_B = 2
T_DEV = 4
PROBES = 64
NCOV = 256
OBS_DEV = 2048
ITERS = 4
NODES_DEV = 1024


relaxation = 0.6


def with_halo(array, sides, width):
    for axis, dim in sides:
        peers, length = (lax.axis_size(axis), array.shape[dim])
        up = [(i, (i + 1) % peers) for i in range(peers - 1)]
        down = [(j, i) for i, j in up]
        last = lax.slice_in_dim(array, length - width, length, axis=dim)
        initial = lax.slice_in_dim(array, 0, width, axis=dim)
        before = lax.ppermute(last, axis, up)
        after = lax.ppermute(initial, axis, down)
        array = jnp.concatenate([before, array, after], axis=dim)
    return array


def shards(
    probe_field,
    kappa,
    theta_space,
    theta_time,
    diag_blocks,
    off_blocks,
    block_cols,
    halo_needs,
    covariates,
    obs_owner,
    obs_cell,
    svc_coef,
):
    space_count = lax.axis_size("space")
    columns = probe_field.shape[1]
    width_local = NB_DEV + 2 * HALO_B
    probe_vals = probe_field.astype(jnp.float32)
    eye = jnp.arange(BLOCK)[:, None] == jnp.arange(BLOCK)[None, :]
    sdiag = jnp.sum(jnp.where(eye[None], diag_blocks.astype(jnp.float32), 0.0), axis=2).reshape(
        NODES_DEV
    )
    scale_space = jnp.repeat(theta_space, PROBES)[None, :]
    scale_time = jnp.repeat(theta_time, PROBES)[None, :]
    base_diag = scale_space * sdiag[:, None] + 2.0 * scale_time + kappa[:, None]
    local_ids = jnp.arange(width_local, dtype=jnp.int32)
    picks = (block_cols[:, :, None] == local_ids[None, None, :]).astype(jnp.float32)
    own_pick = (jnp.arange(NB_DEV, dtype=jnp.int32)[:, None] == local_ids[None, :]).astype(
        jnp.float32
    )
    combined = jnp.einsum("bkm,bkij->bimj", picks, off_blocks.astype(jnp.float32))
    combined = combined + jnp.einsum("bm,bij->bimj", own_pick, diag_blocks.astype(jnp.float32))
    combined = combined.astype(jnp.bfloat16).reshape(NODES_DEV, width_local * BLOCK)
    own_part = combined[:, :NODES_DEV]
    lower_part = combined[:, NODES_DEV : NODES_DEV + HALO_B * BLOCK]
    upper_part = combined[:, NODES_DEV + HALO_B * BLOCK :]
    own_t, lower_t, upper_t = own_part.T, lower_part.T, upper_part.T

    space_index = lax.axis_index("space")
    up = [(i, i + 1) for i in range(space_count - 1)]
    down = [(i + 1, i) for i in range(space_count - 1)]
    upper_wants = lax.ppermute(halo_needs[:HALO_B], "space", down)
    lower_wants = lax.ppermute(halo_needs[HALO_B:], "space", up)

    def pick_blocks(field, wanted):
        return jnp.concatenate(
            [lax.dynamic_slice_in_dim(field, wanted[j] * BLOCK, BLOCK, axis=0) for j in range(HALO_B)],
            axis=0,
        )

    def spatial(field):
        lower = lax.ppermute(pick_blocks(field, upper_wants), "space", up)
        upper = lax.ppermute(pick_blocks(field, lower_wants), "space", down)
        total = jnp.dot(field.T, own_t, preferred_element_type=jnp.float32)
        total = total + jnp.dot(lower.T, lower_t, preferred_element_type=jnp.float32)
        total = total + jnp.dot(upper.T, upper_t, preferred_element_type=jnp.float32)
        return total.T

    def temporal(field):
        arrived = with_halo(field, (("tm", 1),), PROBES)
        return (
            2.0 * field.astype(jnp.float32)
            - arrived[:, :columns].astype(jnp.float32)
            - arrived[:, 2 * PROBES :].astype(jnp.float32)
        )

    solution = relaxation * probe_vals / base_diag
    rounded = lax.optimization_barrier(solution.astype(jnp.bfloat16))
    first_space = spatial(rounded)
    first_time = temporal(rounded)
    nodes_dev = svc_coef.shape[0]
    tables = [svc_coef] + [
        lax.ppermute(svc_coef, "space", [(i, (i + k) % space_count) for i in range(space_count)])
        for k in range(1, space_count)
    ]
    svc_all = jnp.concatenate(tables, axis=0)
    owner = obs_owner[:, 0]
    shift = (lax.axis_index("space") - owner) % space_count
    coef_rows = svc_all[shift * nodes_dev + obs_cell // T_DEV]
    eta = jnp.einsum("rc,rc->r", covariates, coef_rows, preferred_element_type=jnp.float32)
    obs_weight = jnp.exp(eta)
    node_ids = owner * nodes_dev + obs_cell // T_DEV
    onehot = (node_ids[:, None] == jnp.arange(space_count * nodes_dev)[None, :]).astype(jnp.bfloat16)
    high = lax.reduce_precision(obs_weight, exponent_bits=8, mantissa_bits=7)
    rest = obs_weight - high
    middle = lax.reduce_precision(rest, exponent_bits=8, mantissa_bits=7)
    low = rest - middle
    in_step = obs_cell[:, None] % T_DEV == jnp.arange(T_DEV)[None, :]
    parts = jnp.concatenate(
        [jnp.where(in_step, piece[:, None], 0.0) for piece in (high, middle, low)], axis=1
    ).astype(jnp.bfloat16)
    sums = lax.dot_general(
        onehot, parts, (((0,), (0,)), ((), ())), preferred_element_type=jnp.float32
    )
    local_counts = (sums[:, :T_DEV] + sums[:, T_DEV : 2 * T_DEV] + sums[:, 2 * T_DEV :]).reshape(
        space_count, nodes_dev * T_DEV
    )
    counted = jnp.sum(
        lax.all_to_all(local_counts, "space", split_axis=0, concat_axis=0, tiled=True), axis=0
    )
    obs_diag = jnp.repeat(counted.reshape(NODES_DEV, T_DEV), PROBES, axis=1)
    full_diag = base_diag + obs_diag
    local_diag = kappa[:, None] + obs_diag
    applied = (
        scale_space * first_space
        + scale_time * first_time
        + local_diag * rounded.astype(jnp.float32)
    )
    solution = solution + relaxation * (probe_vals - applied) / full_diag
    for sweep in range(ITERS - 1):
        rounded = lax.optimization_barrier(solution.astype(jnp.bfloat16))
        applied = (
            scale_space * spatial(rounded)
            + scale_time * temporal(rounded)
            + local_diag * rounded.astype(jnp.float32)
        )
        solution = solution + relaxation * (probe_vals - applied) / full_diag
    rounded = solution.astype(jnp.bfloat16)
    partial_sums = jnp.stack(
        [
            jnp.sum(probe_vals * spatial(rounded), axis=0),
            jnp.sum(probe_vals * temporal(rounded), axis=0),
        ]
    )
    totals = lax.psum(partial_sums, "space")
    grads = totals / (NODES_DEV * space_count)
    return (solution, grads)


def solution(mesh):
    return jax.shard_map(
        shards,
        mesh=mesh,
        in_specs=(
            P("space", "tm"),
            P("space"),
            P("tm"),
            P("tm"),
            P("space", None, None),
            P("space", None, None, None),
            P("space", None),
            P("space"),
            P(("space", "tm"), None),
            P(("space", "tm"), None),
            P(("space", "tm")),
            P("space", None),
        ),
        out_specs=(P("space", "tm"), P(None, "tm")),
        check_vma=False,
    )
```

```python
import jax
import jax.numpy as jnp
from jax import lax
from jax.sharding import PartitionSpec as P

NB_DEV = 8
BLOCK = 128
HALO_B = 2
T_DEV = 4
PROBES = 64
NCOV = 256
OBS_DEV = 2048
ITERS = 4
NODES_DEV = 1024


relaxation = 0.6


def with_halo(array, sides, width):
    for axis, dim in sides:
        peers, length = (lax.axis_size(axis), array.shape[dim])
        up = [(i, (i + 1) % peers) for i in range(peers - 1)]
        down = [(j, i) for i, j in up]
        last = lax.slice_in_dim(array, length - width, length, axis=dim)
        initial = lax.slice_in_dim(array, 0, width, axis=dim)
        before = lax.ppermute(last, axis, up)
        after = lax.ppermute(initial, axis, down)
        array = jnp.concatenate([before, array, after], axis=dim)
    return array


def shards(
    probe_field,
    kappa,
    theta_space,
    theta_time,
    diag_blocks,
    off_blocks,
    block_cols,
    halo_needs,
    covariates,
    obs_owner,
    obs_cell,
    svc_coef,
):
    space_count = lax.axis_size("space")
    columns = probe_field.shape[1]
    width_local = NB_DEV + 2 * HALO_B
    probe_vals = probe_field.astype(jnp.float32)
    eye = jnp.arange(BLOCK)[:, None] == jnp.arange(BLOCK)[None, :]
    sdiag = jnp.sum(jnp.where(eye[None], diag_blocks.astype(jnp.float32), 0.0), axis=2).reshape(
        NODES_DEV
    )
    scale_space = jnp.repeat(theta_space, PROBES)[None, :]
    scale_time = jnp.repeat(theta_time, PROBES)[None, :]
    base_diag = scale_space * sdiag[:, None] + 2.0 * scale_time + kappa[:, None]
    local_ids = jnp.arange(width_local, dtype=jnp.int32)
    picks = (block_cols[:, :, None] == local_ids[None, None, :]).astype(jnp.float32)
    own_pick = (jnp.arange(NB_DEV, dtype=jnp.int32)[:, None] == local_ids[None, :]).astype(
        jnp.float32
    )
    combined = jnp.einsum("bkm,bkij->bimj", picks, off_blocks.astype(jnp.float32))
    combined = combined + jnp.einsum("bm,bij->bimj", own_pick, diag_blocks.astype(jnp.float32))
    combined = combined.astype(jnp.bfloat16).reshape(NODES_DEV, width_local * BLOCK)
    own_part = combined[:, :NODES_DEV]
    lower_part = combined[:, NODES_DEV : NODES_DEV + HALO_B * BLOCK]
    upper_part = combined[:, NODES_DEV + HALO_B * BLOCK :]
    own_t, lower_t, upper_t = own_part.T, lower_part.T, upper_part.T

    space_index = lax.axis_index("space")
    up = [(i, i + 1) for i in range(space_count - 1)]
    down = [(i + 1, i) for i in range(space_count - 1)]
    upper_wants = lax.ppermute(halo_needs[:HALO_B], "space", down)
    lower_wants = lax.ppermute(halo_needs[HALO_B:], "space", up)

    def pick_blocks(field, wanted):
        return jnp.concatenate(
            [lax.dynamic_slice_in_dim(field, wanted[j] * BLOCK, BLOCK, axis=0) for j in range(HALO_B)],
            axis=0,
        )

    def spatial(field):
        lower = lax.ppermute(pick_blocks(field, upper_wants), "space", up)
        upper = lax.ppermute(pick_blocks(field, lower_wants), "space", down)
        total = jnp.dot(field.T, own_t, preferred_element_type=jnp.float32)
        total = total + jnp.dot(lower.T, lower_t, preferred_element_type=jnp.float32)
        total = total + jnp.dot(upper.T, upper_t, preferred_element_type=jnp.float32)
        return total.T

    def temporal(field):
        arrived = with_halo(field, (("tm", 1),), PROBES)
        return (
            2.0 * field.astype(jnp.float32)
            - arrived[:, :columns].astype(jnp.float32)
            - arrived[:, 2 * PROBES :].astype(jnp.float32)
        )

    solution = relaxation * probe_vals / base_diag
    rounded = lax.optimization_barrier(solution.astype(jnp.bfloat16))
    first_space = spatial(rounded)
    first_time = temporal(rounded)
    nodes_dev = svc_coef.shape[0]
    tables = [svc_coef] + [
        lax.ppermute(svc_coef, "space", [(i, (i + k) % space_count) for i in range(space_count)])
        for k in range(1, space_count)
    ]
    svc_all = jnp.concatenate(tables, axis=0)
    owner = obs_owner[:, 0]
    shift = (lax.axis_index("space") - owner) % space_count
    coef_rows = svc_all[shift * nodes_dev + obs_cell // T_DEV]
    eta = jnp.einsum("rc,rc->r", covariates, coef_rows, preferred_element_type=jnp.float32)
    obs_weight = jnp.exp(eta)
    node_ids = owner * nodes_dev + obs_cell // T_DEV
    onehot = (node_ids[:, None] == jnp.arange(space_count * nodes_dev)[None, :]).astype(jnp.bfloat16)
    high = lax.reduce_precision(obs_weight, exponent_bits=8, mantissa_bits=7)
    rest = obs_weight - high
    middle = lax.reduce_precision(rest, exponent_bits=8, mantissa_bits=7)
    low = rest - middle
    in_step = obs_cell[:, None] % T_DEV == jnp.arange(T_DEV)[None, :]
    parts = jnp.concatenate(
        [jnp.where(in_step, piece[:, None], 0.0) for piece in (high, middle, low)], axis=1
    ).astype(jnp.bfloat16)
    sums = lax.dot_general(
        parts, onehot, (((0,), (0,)), ((), ())), preferred_element_type=jnp.float32
    )
    step_counts = sums[:T_DEV] + sums[T_DEV : 2 * T_DEV] + sums[2 * T_DEV :]
    local_counts = step_counts.reshape(T_DEV, space_count, nodes_dev).transpose(1, 0, 2)
    counted = jnp.sum(
        lax.all_to_all(local_counts, "space", split_axis=0, concat_axis=0, tiled=True), axis=0
    )
    obs_diag = jnp.repeat(counted, PROBES, axis=0).T
    full_diag = base_diag + obs_diag
    local_diag = kappa[:, None] + obs_diag
    applied = (
        scale_space * first_space
        + scale_time * first_time
        + local_diag * rounded.astype(jnp.float32)
    )
    solution = solution + relaxation * (probe_vals - applied) / full_diag
    for sweep in range(ITERS - 1):
        rounded = lax.optimization_barrier(solution.astype(jnp.bfloat16))
        applied = (
            scale_space * spatial(rounded)
            + scale_time * temporal(rounded)
            + local_diag * rounded.astype(jnp.float32)
        )
        solution = solution + relaxation * (probe_vals - applied) / full_diag
    rounded = solution.astype(jnp.bfloat16)
    partial_sums = jnp.stack(
        [
            jnp.sum(probe_vals * spatial(rounded), axis=0),
            jnp.sum(probe_vals * temporal(rounded), axis=0),
        ]
    )
    totals = lax.psum(partial_sums, "space")
    grads = totals / (NODES_DEV * space_count)
    return (solution, grads)


def solution(mesh):
    return jax.shard_map(
        shards,
        mesh=mesh,
        in_specs=(
            P("space", "tm"),
            P("space"),
            P("tm"),
            P("tm"),
            P("space", None, None),
            P("space", None, None, None),
            P("space", None),
            P("space"),
            P(("space", "tm"), None),
            P(("space", "tm"), None),
            P(("space", "tm")),
            P("space", None),
        ),
        out_specs=(P("space", "tm"), P(None, "tm")),
        check_vma=False,
    )
```

```python
import jax
import jax.numpy as jnp
from jax import lax
from jax.sharding import PartitionSpec as P

NB_DEV = 8
BLOCK = 128
HALO_B = 2
T_DEV = 4
PROBES = 64
NCOV = 256
OBS_DEV = 2048
ITERS = 4
NODES_DEV = 1024


relaxation = 0.6


def with_halo(array, sides, width):
    for axis, dim in sides:
        peers, length = (lax.axis_size(axis), array.shape[dim])
        up = [(i, (i + 1) % peers) for i in range(peers - 1)]
        down = [(j, i) for i, j in up]
        last = lax.slice_in_dim(array, length - width, length, axis=dim)
        initial = lax.slice_in_dim(array, 0, width, axis=dim)
        before = lax.ppermute(last, axis, up)
        after = lax.ppermute(initial, axis, down)
        array = jnp.concatenate([before, array, after], axis=dim)
    return array


def shards(
    probe_field,
    kappa,
    theta_space,
    theta_time,
    diag_blocks,
    off_blocks,
    block_cols,
    halo_needs,
    covariates,
    obs_owner,
    obs_cell,
    svc_coef,
):
    space_count = lax.axis_size("space")
    columns = probe_field.shape[1]
    width_local = NB_DEV + 2 * HALO_B
    probe_vals = probe_field.astype(jnp.float32)
    eye = jnp.arange(BLOCK)[:, None] == jnp.arange(BLOCK)[None, :]
    sdiag = jnp.sum(jnp.where(eye[None], diag_blocks.astype(jnp.float32), 0.0), axis=2).reshape(
        NODES_DEV
    )
    scale_space = jnp.repeat(theta_space, PROBES)[None, :]
    scale_time = jnp.repeat(theta_time, PROBES)[None, :]
    base_diag = scale_space * sdiag[:, None] + 2.0 * scale_time + kappa[:, None]
    local_ids = jnp.arange(width_local, dtype=jnp.int32)
    picks = (block_cols[:, :, None] == local_ids[None, None, :]).astype(jnp.float32)
    own_pick = (jnp.arange(NB_DEV, dtype=jnp.int32)[:, None] == local_ids[None, :]).astype(
        jnp.float32
    )
    combined = jnp.einsum("bkm,bkij->bimj", picks, off_blocks.astype(jnp.float32))
    combined = combined + jnp.einsum("bm,bij->bimj", own_pick, diag_blocks.astype(jnp.float32))
    combined = combined.astype(jnp.bfloat16).reshape(NODES_DEV, width_local * BLOCK)
    own_part = combined[:, :NODES_DEV]
    lower_part = combined[:, NODES_DEV : NODES_DEV + HALO_B * BLOCK]
    upper_part = combined[:, NODES_DEV + HALO_B * BLOCK :]
    own_t, lower_t, upper_t = own_part.T, lower_part.T, upper_part.T

    space_index = lax.axis_index("space")
    nodes_dev = svc_coef.shape[0]
    up = [(i, i + 1) for i in range(space_count - 1)]
    down = [(i + 1, i) for i in range(space_count - 1)]
    pad_rows = 16
    needs_rows = jnp.zeros((pad_rows, svc_coef.shape[1]), jnp.bfloat16)
    needs_rows = needs_rows.at[0, : halo_needs.shape[0]].set(halo_needs.astype(jnp.bfloat16))
    extended = jnp.concatenate([svc_coef, needs_rows], axis=0)
    tables = [extended] + [
        lax.ppermute(extended, "space", [(i, (i + k) % space_count) for i in range(space_count)])
        for k in range(1, space_count)
    ]
    lower_wants = tables[1][nodes_dev, HALO_B : 2 * HALO_B].astype(jnp.int32)
    upper_wants = tables[space_count - 1][nodes_dev, :HALO_B].astype(jnp.int32)

    def pick_blocks(field, wanted):
        return jnp.concatenate(
            [lax.dynamic_slice_in_dim(field, wanted[j] * BLOCK, BLOCK, axis=0) for j in range(HALO_B)],
            axis=0,
        )

    def spatial(field):
        lower = lax.ppermute(pick_blocks(field, upper_wants), "space", up)
        upper = lax.ppermute(pick_blocks(field, lower_wants), "space", down)
        total = jnp.dot(field.T, own_t, preferred_element_type=jnp.float32)
        total = total + jnp.dot(lower.T, lower_t, preferred_element_type=jnp.float32)
        total = total + jnp.dot(upper.T, upper_t, preferred_element_type=jnp.float32)
        return total.T

    def temporal(field):
        arrived = with_halo(field, (("tm", 1),), PROBES)
        return (
            2.0 * field.astype(jnp.float32)
            - arrived[:, :columns].astype(jnp.float32)
            - arrived[:, 2 * PROBES :].astype(jnp.float32)
        )

    solution = relaxation * probe_vals / base_diag
    rounded = lax.optimization_barrier(solution.astype(jnp.bfloat16))
    first_space = spatial(rounded)
    first_time = temporal(rounded)
    svc_all = jnp.concatenate(tables, axis=0)
    owner = obs_owner[:, 0]
    shift = (lax.axis_index("space") - owner) % space_count
    coef_rows = svc_all[shift * (nodes_dev + pad_rows) + obs_cell // T_DEV]
    eta = jnp.einsum("rc,rc->r", covariates, coef_rows, preferred_element_type=jnp.float32)
    obs_weight = jnp.exp(eta)
    node_ids = owner * nodes_dev + obs_cell // T_DEV
    onehot = (node_ids[:, None] == jnp.arange(space_count * nodes_dev)[None, :]).astype(jnp.bfloat16)
    high = lax.reduce_precision(obs_weight, exponent_bits=8, mantissa_bits=7)
    rest = obs_weight - high
    middle = lax.reduce_precision(rest, exponent_bits=8, mantissa_bits=7)
    low = rest - middle
    in_step = obs_cell[:, None] % T_DEV == jnp.arange(T_DEV)[None, :]
    parts = jnp.concatenate(
        [jnp.where(in_step, piece[:, None], 0.0) for piece in (high, middle, low)], axis=1
    ).astype(jnp.bfloat16)
    sums = lax.dot_general(
        parts, onehot, (((0,), (0,)), ((), ())), preferred_element_type=jnp.float32
    )
    step_counts = sums[:T_DEV] + sums[T_DEV : 2 * T_DEV] + sums[2 * T_DEV :]
    local_counts = step_counts.reshape(T_DEV, space_count, nodes_dev).transpose(1, 0, 2)
    counted = jnp.sum(
        lax.all_to_all(local_counts, "space", split_axis=0, concat_axis=0, tiled=True), axis=0
    )
    obs_diag = jnp.repeat(counted, PROBES, axis=0).T
    full_diag = base_diag + obs_diag
    local_diag = kappa[:, None] + obs_diag
    applied = (
        scale_space * first_space
        + scale_time * first_time
        + local_diag * rounded.astype(jnp.float32)
    )
    solution = solution + relaxation * (probe_vals - applied) / full_diag
    for sweep in range(ITERS - 1):
        rounded = lax.optimization_barrier(solution.astype(jnp.bfloat16))
        applied = (
            scale_space * spatial(rounded)
            + scale_time * temporal(rounded)
            + local_diag * rounded.astype(jnp.float32)
        )
        solution = solution + relaxation * (probe_vals - applied) / full_diag
    rounded = solution.astype(jnp.bfloat16)
    partial_sums = jnp.stack(
        [
            jnp.sum(probe_vals * spatial(rounded), axis=0),
            jnp.sum(probe_vals * temporal(rounded), axis=0),
        ]
    )
    totals = lax.psum(partial_sums, "space")
    grads = totals / (NODES_DEV * space_count)
    return (solution, grads)


def solution(mesh):
    return jax.shard_map(
        shards,
        mesh=mesh,
        in_specs=(
            P("space", "tm"),
            P("space"),
            P("tm"),
            P("tm"),
            P("space", None, None),
            P("space", None, None, None),
            P("space", None),
            P("space"),
            P(("space", "tm"), None),
            P(("space", "tm"), None),
            P(("space", "tm")),
            P("space", None),
        ),
        out_specs=(P("space", "tm"), P(None, "tm")),
        check_vma=False,
    )
```

```python
import jax
import jax.numpy as jnp
from jax import lax
from jax.sharding import PartitionSpec as P

NB_DEV = 8
BLOCK = 128
HALO_B = 2
T_DEV = 4
PROBES = 64
NCOV = 256
OBS_DEV = 2048
ITERS = 4
NODES_DEV = 1024


relaxation = 0.6


def with_halo(array, sides, width):
    for axis, dim in sides:
        peers, length = (lax.axis_size(axis), array.shape[dim])
        up = [(i, (i + 1) % peers) for i in range(peers - 1)]
        down = [(j, i) for i, j in up]
        last = lax.slice_in_dim(array, length - width, length, axis=dim)
        initial = lax.slice_in_dim(array, 0, width, axis=dim)
        before = lax.ppermute(last, axis, up)
        after = lax.ppermute(initial, axis, down)
        array = jnp.concatenate([before, array, after], axis=dim)
    return array


def shards(
    probe_field,
    kappa,
    theta_space,
    theta_time,
    diag_blocks,
    off_blocks,
    block_cols,
    halo_needs,
    covariates,
    obs_owner,
    obs_cell,
    svc_coef,
):
    space_count = lax.axis_size("space")
    columns = probe_field.shape[1]
    width_local = NB_DEV + 2 * HALO_B
    probe_vals = probe_field.astype(jnp.float32)
    eye = jnp.arange(BLOCK)[:, None] == jnp.arange(BLOCK)[None, :]
    sdiag = jnp.sum(jnp.where(eye[None], diag_blocks.astype(jnp.float32), 0.0), axis=2).reshape(
        NODES_DEV
    )
    scale_space = jnp.repeat(theta_space, PROBES)[None, :]
    scale_time = jnp.repeat(theta_time, PROBES)[None, :]
    base_diag = scale_space * sdiag[:, None] + 2.0 * scale_time + kappa[:, None]
    local_ids = jnp.arange(width_local, dtype=jnp.int32)
    picks = (block_cols[:, :, None] == local_ids[None, None, :]).astype(jnp.float32)
    own_pick = (jnp.arange(NB_DEV, dtype=jnp.int32)[:, None] == local_ids[None, :]).astype(
        jnp.float32
    )
    combined = jnp.einsum("bkm,bkij->bimj", picks, off_blocks.astype(jnp.float32))
    combined = combined + jnp.einsum("bm,bij->bimj", own_pick, diag_blocks.astype(jnp.float32))
    combined = combined.astype(jnp.bfloat16).reshape(NODES_DEV, width_local * BLOCK)
    own_part = combined[:, :NODES_DEV]
    lower_part = combined[:, NODES_DEV : NODES_DEV + HALO_B * BLOCK]
    upper_part = combined[:, NODES_DEV + HALO_B * BLOCK :]
    own_t, lower_t, upper_t = own_part.T, lower_part.T, upper_part.T

    space_index = lax.axis_index("space")
    up = [(i, i + 1) for i in range(space_count - 1)]
    down = [(i + 1, i) for i in range(space_count - 1)]
    upper_wants = lax.ppermute(halo_needs[:HALO_B], "space", down)
    lower_wants = lax.ppermute(halo_needs[HALO_B:], "space", up)

    def pick_blocks(field, wanted):
        return jnp.concatenate(
            [lax.dynamic_slice_in_dim(field, wanted[j] * BLOCK, BLOCK, axis=0) for j in range(HALO_B)],
            axis=0,
        )

    def spatial(field):
        lower = lax.ppermute(pick_blocks(field, upper_wants), "space", up)
        upper = lax.ppermute(pick_blocks(field, lower_wants), "space", down)
        total = jnp.dot(field.T, own_t, preferred_element_type=jnp.float32)
        total = total + jnp.dot(lower.T, lower_t, preferred_element_type=jnp.float32)
        total = total + jnp.dot(upper.T, upper_t, preferred_element_type=jnp.float32)
        return total.T

    def temporal(field):
        arrived = with_halo(field, (("tm", 1),), PROBES)
        return (
            2.0 * field.astype(jnp.float32)
            - arrived[:, :columns].astype(jnp.float32)
            - arrived[:, 2 * PROBES :].astype(jnp.float32)
        )

    solution = relaxation * probe_vals / base_diag
    rounded = lax.optimization_barrier(solution.astype(jnp.bfloat16))
    first_space = spatial(rounded)
    first_time = temporal(rounded)
    nodes_dev = svc_coef.shape[0]
    tables = [svc_coef] + [
        lax.ppermute(svc_coef, "space", [(i, (i + k) % space_count) for i in range(space_count)])
        for k in range(1, space_count)
    ]
    svc_all = jnp.concatenate(tables, axis=0)
    owner = obs_owner[:, 0]
    shift = (lax.axis_index("space") - owner) % space_count
    coef_rows = svc_all[shift * nodes_dev + obs_cell // T_DEV]
    eta = jnp.einsum("rc,rc->r", covariates, coef_rows, preferred_element_type=jnp.float32)
    obs_weight = jnp.exp(eta)
    onehot = (obs_cell[:, None] // T_DEV == jnp.arange(nodes_dev)[None, :]).astype(jnp.bfloat16)
    high = lax.reduce_precision(obs_weight, exponent_bits=8, mantissa_bits=7)
    rest = obs_weight - high
    middle = lax.reduce_precision(rest, exponent_bits=8, mantissa_bits=7)
    low = rest - middle
    slot = owner * T_DEV + obs_cell % T_DEV
    in_slot = slot[:, None] == jnp.arange(space_count * T_DEV)[None, :]
    parts = jnp.concatenate(
        [jnp.where(in_slot, piece[:, None], 0.0) for piece in (high, middle, low)], axis=1
    ).astype(jnp.bfloat16)
    sums = lax.dot_general(
        parts, onehot, (((0,), (0,)), ((), ())), preferred_element_type=jnp.float32
    ).reshape(3, space_count, T_DEV, nodes_dev)
    local_counts = sums[0] + sums[1] + sums[2]
    counted = jnp.sum(
        lax.all_to_all(local_counts, "space", split_axis=0, concat_axis=0, tiled=True), axis=0
    )
    obs_diag = jnp.repeat(counted, PROBES, axis=0).T
    full_diag = base_diag + obs_diag
    local_diag = kappa[:, None] + obs_diag
    applied = (
        scale_space * first_space
        + scale_time * first_time
        + local_diag * rounded.astype(jnp.float32)
    )
    solution = solution + relaxation * (probe_vals - applied) / full_diag
    for sweep in range(ITERS - 1):
        rounded = lax.optimization_barrier(solution.astype(jnp.bfloat16))
        applied = (
            scale_space * spatial(rounded)
            + scale_time * temporal(rounded)
            + local_diag * rounded.astype(jnp.float32)
        )
        solution = solution + relaxation * (probe_vals - applied) / full_diag
    rounded = solution.astype(jnp.bfloat16)
    partial_sums = jnp.stack(
        [
            jnp.sum(probe_vals * spatial(rounded), axis=0),
            jnp.sum(probe_vals * temporal(rounded), axis=0),
        ]
    )
    totals = lax.psum(partial_sums, "space")
    grads = totals / (NODES_DEV * space_count)
    return (solution, grads)


def solution(mesh):
    return jax.shard_map(
        shards,
        mesh=mesh,
        in_specs=(
            P("space", "tm"),
            P("space"),
            P("tm"),
            P("tm"),
            P("space", None, None),
            P("space", None, None, None),
            P("space", None),
            P("space"),
            P(("space", "tm"), None),
            P(("space", "tm"), None),
            P(("space", "tm")),
            P("space", None),
        ),
        out_specs=(P("space", "tm"), P(None, "tm")),
        check_vma=False,
    )
```

```python
import jax
import jax.numpy as jnp
from jax import lax
from jax.sharding import PartitionSpec as P

NB_DEV = 8
BLOCK = 128
HALO_B = 2
T_DEV = 4
PROBES = 64
NCOV = 256
OBS_DEV = 2048
ITERS = 4
NODES_DEV = 1024


relaxation = 0.6


def with_halo(array, sides, width):
    for axis, dim in sides:
        peers, length = (lax.axis_size(axis), array.shape[dim])
        up = [(i, (i + 1) % peers) for i in range(peers - 1)]
        down = [(j, i) for i, j in up]
        last = lax.slice_in_dim(array, length - width, length, axis=dim)
        initial = lax.slice_in_dim(array, 0, width, axis=dim)
        before = lax.ppermute(last, axis, up)
        after = lax.ppermute(initial, axis, down)
        array = jnp.concatenate([before, array, after], axis=dim)
    return array


def shards(
    probe_field,
    kappa,
    theta_space,
    theta_time,
    diag_blocks,
    off_blocks,
    block_cols,
    halo_needs,
    covariates,
    obs_owner,
    obs_cell,
    svc_coef,
):
    space_count = lax.axis_size("space")
    columns = probe_field.shape[1]
    width_local = NB_DEV + 2 * HALO_B
    probe_vals = probe_field.astype(jnp.float32)
    eye = jnp.arange(BLOCK)[:, None] == jnp.arange(BLOCK)[None, :]
    sdiag = jnp.sum(jnp.where(eye[None], diag_blocks.astype(jnp.float32), 0.0), axis=2).reshape(
        NODES_DEV
    )
    scale_space = jnp.repeat(theta_space, PROBES)[None, :]
    scale_time = jnp.repeat(theta_time, PROBES)[None, :]
    base_diag = scale_space * sdiag[:, None] + 2.0 * scale_time + kappa[:, None]
    local_ids = jnp.arange(width_local, dtype=jnp.int32)
    picks = (block_cols[:, :, None] == local_ids[None, None, :]).astype(jnp.float32)
    own_pick = (jnp.arange(NB_DEV, dtype=jnp.int32)[:, None] == local_ids[None, :]).astype(
        jnp.float32
    )
    combined = jnp.einsum("bkm,bkij->bimj", picks, off_blocks.astype(jnp.float32))
    combined = combined + jnp.einsum("bm,bij->bimj", own_pick, diag_blocks.astype(jnp.float32))
    combined = combined.astype(jnp.bfloat16).reshape(NODES_DEV, width_local * BLOCK)
    own_part = combined[:, :NODES_DEV]
    lower_part = combined[:, NODES_DEV : NODES_DEV + HALO_B * BLOCK]
    upper_part = combined[:, NODES_DEV + HALO_B * BLOCK :]
    own_t, lower_t, upper_t = own_part.T, lower_part.T, upper_part.T

    space_index = lax.axis_index("space")
    up = [(i, i + 1) for i in range(space_count - 1)]
    down = [(i + 1, i) for i in range(space_count - 1)]
    upper_wants = lax.ppermute(halo_needs[:HALO_B], "space", down)
    lower_wants = lax.ppermute(halo_needs[HALO_B:], "space", up)

    def pick_blocks(field, wanted):
        return jnp.concatenate(
            [lax.dynamic_slice_in_dim(field, wanted[j] * BLOCK, BLOCK, axis=0) for j in range(HALO_B)],
            axis=0,
        )

    def spatial(field):
        lower = lax.ppermute(pick_blocks(field, upper_wants), "space", up)
        upper = lax.ppermute(pick_blocks(field, lower_wants), "space", down)
        total = jnp.dot(field.T, own_t, preferred_element_type=jnp.float32)
        total = total + jnp.dot(lower.T, lower_t, preferred_element_type=jnp.float32)
        total = total + jnp.dot(upper.T, upper_t, preferred_element_type=jnp.float32)
        return total.T

    def temporal(field):
        arrived = with_halo(field, (("tm", 1),), PROBES)
        return (
            2.0 * field.astype(jnp.float32)
            - arrived[:, :columns].astype(jnp.float32)
            - arrived[:, 2 * PROBES :].astype(jnp.float32)
        )

    def add_block(whole, part, block):
        start = block * BLOCK
        current = lax.dynamic_slice_in_dim(whole, start, BLOCK, axis=0)
        return lax.dynamic_update_slice_in_dim(whole, current + part, start, axis=0)

    probe_space = jnp.dot(own_part.T, probe_field, preferred_element_type=jnp.float32)
    to_lower = jnp.dot(lower_part.T, probe_field, preferred_element_type=jnp.float32)
    to_upper = jnp.dot(upper_part.T, probe_field, preferred_element_type=jnp.float32)
    from_upper = lax.ppermute(to_lower, "space", down)
    from_lower = lax.ppermute(to_upper, "space", up)
    for j in range(HALO_B):
        rows = slice(j * BLOCK, (j + 1) * BLOCK)
        probe_space = add_block(probe_space, from_upper[rows], upper_wants[j])
        probe_space = add_block(probe_space, from_lower[rows], lower_wants[j])

    solution = relaxation * probe_vals / base_diag
    rounded = lax.optimization_barrier(solution.astype(jnp.bfloat16))
    first_space = spatial(rounded)
    first_time = temporal(rounded)
    nodes_dev = svc_coef.shape[0]
    tables = [svc_coef] + [
        lax.ppermute(svc_coef, "space", [(i, (i + k) % space_count) for i in range(space_count)])
        for k in range(1, space_count)
    ]
    svc_all = jnp.concatenate(tables, axis=0)
    owner = obs_owner[:, 0]
    shift = (lax.axis_index("space") - owner) % space_count
    coef_rows = svc_all[shift * nodes_dev + obs_cell // T_DEV]
    eta = jnp.einsum("rc,rc->r", covariates, coef_rows, preferred_element_type=jnp.float32)
    obs_weight = jnp.exp(eta)
    onehot = (obs_cell[:, None] // T_DEV == jnp.arange(nodes_dev)[None, :]).astype(jnp.bfloat16)
    high = lax.reduce_precision(obs_weight, exponent_bits=8, mantissa_bits=7)
    rest = obs_weight - high
    middle = lax.reduce_precision(rest, exponent_bits=8, mantissa_bits=7)
    low = rest - middle
    slot = owner * T_DEV + obs_cell % T_DEV
    in_slot = slot[:, None] == jnp.arange(space_count * T_DEV)[None, :]
    parts = jnp.concatenate(
        [jnp.where(in_slot, piece[:, None], 0.0) for piece in (high, middle, low)], axis=1
    ).astype(jnp.bfloat16)
    sums = lax.dot_general(
        parts, onehot, (((0,), (0,)), ((), ())), preferred_element_type=jnp.float32
    ).reshape(3, space_count, T_DEV, nodes_dev)
    local_counts = sums[0] + sums[1] + sums[2]
    counted = jnp.sum(
        lax.all_to_all(local_counts, "space", split_axis=0, concat_axis=0, tiled=True), axis=0
    )
    obs_diag = jnp.repeat(counted, PROBES, axis=0).T
    full_diag = base_diag + obs_diag
    local_diag = kappa[:, None] + obs_diag
    applied = (
        scale_space * first_space
        + scale_time * first_time
        + local_diag * rounded.astype(jnp.float32)
    )
    solution = solution + relaxation * (probe_vals - applied) / full_diag
    for sweep in range(ITERS - 1):
        rounded = lax.optimization_barrier(solution.astype(jnp.bfloat16))
        applied = (
            scale_space * spatial(rounded)
            + scale_time * temporal(rounded)
            + local_diag * rounded.astype(jnp.float32)
        )
        solution = solution + relaxation * (probe_vals - applied) / full_diag
    rounded = solution.astype(jnp.bfloat16)
    partial_sums = jnp.stack(
        [
            jnp.sum(probe_space * rounded.astype(jnp.float32), axis=0),
            jnp.sum(probe_vals * temporal(rounded), axis=0),
        ]
    )
    totals = lax.psum(partial_sums, "space")
    grads = totals / (NODES_DEV * space_count)
    return (solution, grads)


def solution(mesh):
    return jax.shard_map(
        shards,
        mesh=mesh,
        in_specs=(
            P("space", "tm"),
            P("space"),
            P("tm"),
            P("tm"),
            P("space", None, None),
            P("space", None, None, None),
            P("space", None),
            P("space"),
            P(("space", "tm"), None),
            P(("space", "tm"), None),
            P(("space", "tm")),
            P("space", None),
        ),
        out_specs=(P("space", "tm"), P(None, "tm")),
        check_vma=False,
    )
```

```python
import jax
import jax.numpy as jnp
from jax import lax
from jax.sharding import PartitionSpec as P

NB_DEV = 8
BLOCK = 128
HALO_B = 2
T_DEV = 4
PROBES = 64
NCOV = 256
OBS_DEV = 2048
ITERS = 4
NODES_DEV = 1024


relaxation = 0.6


def with_halo(array, sides, width):
    for axis, dim in sides:
        peers, length = (lax.axis_size(axis), array.shape[dim])
        up = [(i, (i + 1) % peers) for i in range(peers - 1)]
        down = [(j, i) for i, j in up]
        last = lax.slice_in_dim(array, length - width, length, axis=dim)
        initial = lax.slice_in_dim(array, 0, width, axis=dim)
        before = lax.ppermute(last, axis, up)
        after = lax.ppermute(initial, axis, down)
        array = jnp.concatenate([before, array, after], axis=dim)
    return array


def shards(
    probe_field,
    kappa,
    theta_space,
    theta_time,
    diag_blocks,
    off_blocks,
    block_cols,
    halo_needs,
    covariates,
    obs_owner,
    obs_cell,
    svc_coef,
):
    space_count = lax.axis_size("space")
    columns = probe_field.shape[1]
    width_local = NB_DEV + 2 * HALO_B
    probe_vals = probe_field.astype(jnp.float32)
    eye = jnp.arange(BLOCK)[:, None] == jnp.arange(BLOCK)[None, :]
    sdiag = jnp.sum(jnp.where(eye[None], diag_blocks.astype(jnp.float32), 0.0), axis=2).reshape(
        NODES_DEV
    )
    scale_space = jnp.repeat(theta_space, PROBES)[None, :]
    scale_time = jnp.repeat(theta_time, PROBES)[None, :]
    base_diag = scale_space * sdiag[:, None] + 2.0 * scale_time + kappa[:, None]
    local_ids = jnp.arange(width_local, dtype=jnp.int32)
    picks = (block_cols[:, :, None] == local_ids[None, None, :]).astype(jnp.float32)
    own_pick = (jnp.arange(NB_DEV, dtype=jnp.int32)[:, None] == local_ids[None, :]).astype(
        jnp.float32
    )
    combined = jnp.einsum("bkm,bkij->bimj", picks, off_blocks.astype(jnp.float32))
    combined = combined + jnp.einsum("bm,bij->bimj", own_pick, diag_blocks.astype(jnp.float32))
    combined = combined.astype(jnp.bfloat16).reshape(NODES_DEV, width_local * BLOCK)
    own_part = combined[:, :NODES_DEV]
    lower_part = combined[:, NODES_DEV : NODES_DEV + HALO_B * BLOCK]
    upper_part = combined[:, NODES_DEV + HALO_B * BLOCK :]
    own_t, lower_t, upper_t = own_part.T, lower_part.T, upper_part.T

    space_index = lax.axis_index("space")
    up = [(i, i + 1) for i in range(space_count - 1)]
    down = [(i + 1, i) for i in range(space_count - 1)]
    upper_wants = lax.ppermute(halo_needs[:HALO_B], "space", down)
    lower_wants = lax.ppermute(halo_needs[HALO_B:], "space", up)

    def pick_blocks(field, wanted):
        return jnp.concatenate(
            [lax.dynamic_slice_in_dim(field, wanted[j] * BLOCK, BLOCK, axis=0) for j in range(HALO_B)],
            axis=0,
        )

    def spatial(field):
        lower = lax.ppermute(pick_blocks(field, upper_wants), "space", up)
        upper = lax.ppermute(pick_blocks(field, lower_wants), "space", down)
        total = jnp.dot(field.T, own_t, preferred_element_type=jnp.float32)
        total = total + jnp.dot(lower.T, lower_t, preferred_element_type=jnp.float32)
        total = total + jnp.dot(upper.T, upper_t, preferred_element_type=jnp.float32)
        return total.T

    def temporal(field):
        arrived = with_halo(field, (("tm", 1),), PROBES)
        return (
            2.0 * field.astype(jnp.float32)
            - arrived[:, :columns].astype(jnp.float32)
            - arrived[:, 2 * PROBES :].astype(jnp.float32)
        )

    solution = relaxation * probe_vals / base_diag
    rounded = lax.optimization_barrier(solution.astype(jnp.bfloat16))
    first_space = spatial(rounded)
    first_time = temporal(rounded)
    nodes_dev = svc_coef.shape[0]
    tables = [svc_coef] + [
        lax.ppermute(svc_coef, "space", [(i, (i + k) % space_count) for i in range(space_count)])
        for k in range(1, space_count)
    ]
    svc_all = jnp.concatenate(tables, axis=0).astype(jnp.float32)
    owner = obs_owner[:, 0]
    shift = (lax.axis_index("space") - owner) % space_count
    coef_rows = svc_all[shift * nodes_dev + obs_cell // T_DEV]
    eta = jnp.sum(covariates.astype(jnp.float32) * coef_rows, axis=1)
    obs_weight = jnp.exp(eta)
    onehot = (obs_cell[:, None] // T_DEV == jnp.arange(nodes_dev)[None, :]).astype(jnp.bfloat16)
    high = lax.reduce_precision(obs_weight, exponent_bits=8, mantissa_bits=7)
    rest = obs_weight - high
    middle = lax.reduce_precision(rest, exponent_bits=8, mantissa_bits=7)
    low = rest - middle
    slot = owner * T_DEV + obs_cell % T_DEV
    in_slot = slot[:, None] == jnp.arange(space_count * T_DEV)[None, :]
    parts = jnp.concatenate(
        [jnp.where(in_slot, piece[:, None], 0.0) for piece in (high, middle, low)], axis=1
    ).astype(jnp.bfloat16)
    sums = lax.dot_general(
        parts, onehot, (((0,), (0,)), ((), ())), preferred_element_type=jnp.float32
    ).reshape(3, space_count, T_DEV, nodes_dev)
    local_counts = sums[0] + sums[1] + sums[2]
    counted = jnp.sum(
        lax.all_to_all(local_counts, "space", split_axis=0, concat_axis=0, tiled=True), axis=0
    )
    obs_diag = jnp.repeat(counted, PROBES, axis=0).T
    full_diag = base_diag + obs_diag
    local_diag = kappa[:, None] + obs_diag
    applied = (
        scale_space * first_space
        + scale_time * first_time
        + local_diag * rounded.astype(jnp.float32)
    )
    solution = solution + relaxation * (probe_vals - applied) / full_diag
    for sweep in range(ITERS - 1):
        rounded = lax.optimization_barrier(solution.astype(jnp.bfloat16))
        applied = (
            scale_space * spatial(rounded)
            + scale_time * temporal(rounded)
            + local_diag * rounded.astype(jnp.float32)
        )
        solution = solution + relaxation * (probe_vals - applied) / full_diag
    rounded = solution.astype(jnp.bfloat16)
    partial_sums = jnp.stack(
        [
            jnp.sum(probe_vals * spatial(rounded), axis=0),
            jnp.sum(probe_vals * temporal(rounded), axis=0),
        ]
    )
    totals = lax.psum(partial_sums, "space")
    grads = totals / (NODES_DEV * space_count)
    return (solution, grads)


def solution(mesh):
    return jax.shard_map(
        shards,
        mesh=mesh,
        in_specs=(
            P("space", "tm"),
            P("space"),
            P("tm"),
            P("tm"),
            P("space", None, None),
            P("space", None, None, None),
            P("space", None),
            P("space"),
            P(("space", "tm"), None),
            P(("space", "tm"), None),
            P(("space", "tm")),
            P("space", None),
        ),
        out_specs=(P("space", "tm"), P(None, "tm")),
        check_vma=False,
    )
```

```python
import jax
import jax.numpy as jnp
from jax import lax
from jax.sharding import PartitionSpec as P

NB_DEV = 8
BLOCK = 128
HALO_B = 2
T_DEV = 4
PROBES = 64
NCOV = 256
OBS_DEV = 2048
ITERS = 4
NODES_DEV = 1024


relaxation = 0.6


def with_halo(array, sides, width):
    for axis, dim in sides:
        peers, length = (lax.axis_size(axis), array.shape[dim])
        up = [(i, (i + 1) % peers) for i in range(peers - 1)]
        down = [(j, i) for i, j in up]
        last = lax.slice_in_dim(array, length - width, length, axis=dim)
        initial = lax.slice_in_dim(array, 0, width, axis=dim)
        before = lax.ppermute(last, axis, up)
        after = lax.ppermute(initial, axis, down)
        array = jnp.concatenate([before, array, after], axis=dim)
    return array


def shards(
    probe_field,
    kappa,
    theta_space,
    theta_time,
    diag_blocks,
    off_blocks,
    block_cols,
    halo_needs,
    covariates,
    obs_owner,
    obs_cell,
    svc_coef,
):
    space_count = lax.axis_size("space")
    columns = probe_field.shape[1]
    width_local = NB_DEV + 2 * HALO_B
    probe_vals = probe_field.astype(jnp.float32)
    eye = jnp.arange(BLOCK)[:, None] == jnp.arange(BLOCK)[None, :]
    sdiag = jnp.sum(jnp.where(eye[None], diag_blocks.astype(jnp.float32), 0.0), axis=2).reshape(
        NODES_DEV
    )
    scale_space = jnp.repeat(theta_space, PROBES)[None, :]
    scale_time = jnp.repeat(theta_time, PROBES)[None, :]
    base_diag = scale_space * sdiag[:, None] + 2.0 * scale_time + kappa[:, None]
    local_ids = jnp.arange(width_local, dtype=jnp.int32)
    picks = (block_cols[:, :, None] == local_ids[None, None, :]).astype(jnp.float32)
    own_pick = (jnp.arange(NB_DEV, dtype=jnp.int32)[:, None] == local_ids[None, :]).astype(
        jnp.float32
    )
    combined = jnp.einsum("bkm,bkij->bimj", picks, off_blocks.astype(jnp.float32))
    combined = combined + jnp.einsum("bm,bij->bimj", own_pick, diag_blocks.astype(jnp.float32))
    combined = combined.astype(jnp.bfloat16).reshape(NODES_DEV, width_local * BLOCK)
    own_part = combined[:, :NODES_DEV]
    lower_part = combined[:, NODES_DEV : NODES_DEV + HALO_B * BLOCK]
    upper_part = combined[:, NODES_DEV + HALO_B * BLOCK :]
    own_t, lower_t, upper_t = own_part.T, lower_part.T, upper_part.T

    space_index = lax.axis_index("space")
    up = [(i, i + 1) for i in range(space_count - 1)]
    down = [(i + 1, i) for i in range(space_count - 1)]
    upper_wants = lax.ppermute(halo_needs[:HALO_B], "space", down)
    lower_wants = lax.ppermute(halo_needs[HALO_B:], "space", up)

    def pick_blocks(field, wanted):
        return jnp.concatenate(
            [lax.dynamic_slice_in_dim(field, wanted[j] * BLOCK, BLOCK, axis=0) for j in range(HALO_B)],
            axis=0,
        )

    def spatial(field):
        lower = lax.ppermute(pick_blocks(field, upper_wants), "space", up)
        upper = lax.ppermute(pick_blocks(field, lower_wants), "space", down)
        total = jnp.dot(field.T, own_t, preferred_element_type=jnp.float32)
        total = total + jnp.dot(lower.T, lower_t, preferred_element_type=jnp.float32)
        total = total + jnp.dot(upper.T, upper_t, preferred_element_type=jnp.float32)
        return total.T

    def temporal(field):
        arrived = with_halo(field, (("tm", 1),), PROBES)
        return (
            2.0 * field.astype(jnp.float32)
            - arrived[:, :columns].astype(jnp.float32)
            - arrived[:, 2 * PROBES :].astype(jnp.float32)
        )

    solution = relaxation * probe_vals / base_diag
    rounded = lax.optimization_barrier(solution.astype(jnp.bfloat16))
    first_space = spatial(rounded)
    first_time = temporal(rounded)
    nodes_dev = svc_coef.shape[0]
    tables = [svc_coef] + [
        lax.ppermute(svc_coef, "space", [(i, (i + k) % space_count) for i in range(space_count)])
        for k in range(1, space_count)
    ]
    svc_all = jnp.concatenate(tables, axis=0).astype(jnp.float32)
    owner = obs_owner[:, 0]
    shift = (lax.axis_index("space") - owner) % space_count
    coef_rows = svc_all[shift * nodes_dev + obs_cell // T_DEV]
    eta = jnp.sum(covariates.astype(jnp.float32) * coef_rows, axis=1)
    obs_weight = jnp.exp(eta)
    onehot = (obs_cell[:, None] // T_DEV == jnp.arange(nodes_dev)[None, :]).astype(jnp.bfloat16)
    high = lax.reduce_precision(obs_weight, exponent_bits=8, mantissa_bits=7)
    rest = obs_weight - high
    middle = lax.reduce_precision(rest, exponent_bits=8, mantissa_bits=7)
    low = rest - middle
    slot = owner * T_DEV + obs_cell % T_DEV
    in_slot = slot[:, None] == jnp.arange(space_count * T_DEV)[None, :]
    parts = jnp.concatenate(
        [jnp.where(in_slot, piece[:, None], 0.0) for piece in (high, middle, low)], axis=1
    ).astype(jnp.bfloat16)
    sums = lax.dot_general(
        parts, onehot, (((0,), (0,)), ((), ())), preferred_element_type=jnp.float32
    ).reshape(3, space_count, T_DEV, nodes_dev)
    local_counts = sums[0] + sums[1] + sums[2]
    counted = jnp.sum(
        lax.all_to_all(local_counts, "space", split_axis=0, concat_axis=0, tiled=True), axis=0
    )
    obs_diag = jnp.repeat(counted, PROBES, axis=0).T
    full_diag = base_diag + obs_diag
    local_diag = kappa[:, None] + obs_diag
    applied = (
        scale_space * first_space
        + scale_time * first_time
        + local_diag * rounded.astype(jnp.float32)
    )
    solution = solution + relaxation * (probe_vals - applied) / full_diag
    for sweep in range(ITERS - 1):
        rounded = lax.optimization_barrier(solution.astype(jnp.bfloat16))
        applied = (
            scale_space * spatial(rounded)
            + scale_time * temporal(rounded)
            + local_diag * rounded.astype(jnp.float32)
        )
        solution = solution + relaxation * (probe_vals - applied) / full_diag
    rounded = solution.astype(jnp.bfloat16)
    partial_sums = jnp.stack(
        [
            jnp.sum(probe_vals * spatial(rounded), axis=0),
            jnp.sum(probe_vals * temporal(rounded), axis=0),
        ]
    )
    totals = jnp.sum(
        lax.all_to_all(
            jnp.broadcast_to(partial_sums[None], (space_count,) + partial_sums.shape),
            "space", split_axis=0, concat_axis=0, tiled=True,
        ),
        axis=0,
    )
    grads = totals / (NODES_DEV * space_count)
    return (solution, grads)


def solution(mesh):
    return jax.shard_map(
        shards,
        mesh=mesh,
        in_specs=(
            P("space", "tm"),
            P("space"),
            P("tm"),
            P("tm"),
            P("space", None, None),
            P("space", None, None, None),
            P("space", None),
            P("space"),
            P(("space", "tm"), None),
            P(("space", "tm"), None),
            P(("space", "tm")),
            P("space", None),
        ),
        out_specs=(P("space", "tm"), P(None, "tm")),
        check_vma=False,
    )
```

```python
import jax
import jax.numpy as jnp
from jax import lax
from jax.sharding import PartitionSpec as P

NB_DEV = 8
BLOCK = 128
HALO_B = 2
T_DEV = 4
PROBES = 64
NCOV = 256
OBS_DEV = 2048
ITERS = 4
NODES_DEV = 1024


relaxation = 0.6


def with_halo(array, sides, width):
    for axis, dim in sides:
        peers, length = (lax.axis_size(axis), array.shape[dim])
        up = [(i, (i + 1) % peers) for i in range(peers - 1)]
        down = [(j, i) for i, j in up]
        last = lax.slice_in_dim(array, length - width, length, axis=dim)
        initial = lax.slice_in_dim(array, 0, width, axis=dim)
        before = lax.ppermute(last, axis, up)
        after = lax.ppermute(initial, axis, down)
        array = jnp.concatenate([before, array, after], axis=dim)
    return array


def shards(
    probe_field,
    kappa,
    theta_space,
    theta_time,
    diag_blocks,
    off_blocks,
    block_cols,
    halo_needs,
    covariates,
    obs_owner,
    obs_cell,
    svc_coef,
):
    space_count = lax.axis_size("space")
    columns = probe_field.shape[1]
    width_local = NB_DEV + 2 * HALO_B
    probe_vals = probe_field.astype(jnp.float32)
    eye = jnp.arange(BLOCK)[:, None] == jnp.arange(BLOCK)[None, :]
    sdiag = jnp.sum(jnp.where(eye[None], diag_blocks.astype(jnp.float32), 0.0), axis=2).reshape(
        NODES_DEV
    )
    scale_space = jnp.repeat(theta_space, PROBES)[None, :]
    scale_time = jnp.repeat(theta_time, PROBES)[None, :]
    base_diag = scale_space * sdiag[:, None] + 2.0 * scale_time + kappa[:, None]
    local_ids = jnp.arange(width_local, dtype=jnp.int32)
    picks = (block_cols[:, :, None] == local_ids[None, None, :]).astype(jnp.float32)
    own_pick = (jnp.arange(NB_DEV, dtype=jnp.int32)[:, None] == local_ids[None, :]).astype(
        jnp.float32
    )
    combined = jnp.einsum("bkm,bkij->bimj", picks, off_blocks.astype(jnp.float32))
    combined = combined + jnp.einsum("bm,bij->bimj", own_pick, diag_blocks.astype(jnp.float32))
    combined = combined.astype(jnp.bfloat16).reshape(NODES_DEV, width_local * BLOCK)
    own_part = combined[:, :NODES_DEV]
    lower_part = combined[:, NODES_DEV : NODES_DEV + HALO_B * BLOCK]
    upper_part = combined[:, NODES_DEV + HALO_B * BLOCK :]
    own_t, lower_t, upper_t = own_part.T, lower_part.T, upper_part.T

    space_index = lax.axis_index("space")
    up = [(i, i + 1) for i in range(space_count - 1)]
    down = [(i + 1, i) for i in range(space_count - 1)]
    every_needs = lax.all_to_all(
        jnp.broadcast_to(halo_needs[None], (space_count,) + halo_needs.shape),
        "space", split_axis=0, concat_axis=0, tiled=True,
    )
    space_index = lax.axis_index("space")
    upper_wants = every_needs[jnp.minimum(space_index + 1, space_count - 1), :HALO_B]
    lower_wants = every_needs[jnp.maximum(space_index - 1, 0), HALO_B:]

    def pick_blocks(field, wanted):
        return jnp.concatenate(
            [lax.dynamic_slice_in_dim(field, wanted[j] * BLOCK, BLOCK, axis=0) for j in range(HALO_B)],
            axis=0,
        )

    def spatial(field):
        lower = lax.ppermute(pick_blocks(field, upper_wants), "space", up)
        upper = lax.ppermute(pick_blocks(field, lower_wants), "space", down)
        total = jnp.dot(field.T, own_t, preferred_element_type=jnp.float32)
        total = total + jnp.dot(lower.T, lower_t, preferred_element_type=jnp.float32)
        total = total + jnp.dot(upper.T, upper_t, preferred_element_type=jnp.float32)
        return total.T

    def temporal(field):
        arrived = with_halo(field, (("tm", 1),), PROBES)
        return (
            2.0 * field.astype(jnp.float32)
            - arrived[:, :columns].astype(jnp.float32)
            - arrived[:, 2 * PROBES :].astype(jnp.float32)
        )

    solution = relaxation * probe_vals / base_diag
    rounded = lax.optimization_barrier(solution.astype(jnp.bfloat16))
    first_space = spatial(rounded)
    first_time = temporal(rounded)
    nodes_dev = svc_coef.shape[0]
    tables = [svc_coef] + [
        lax.ppermute(svc_coef, "space", [(i, (i + k) % space_count) for i in range(space_count)])
        for k in range(1, space_count)
    ]
    svc_all = jnp.concatenate(tables, axis=0).astype(jnp.float32)
    owner = obs_owner[:, 0]
    shift = (lax.axis_index("space") - owner) % space_count
    coef_rows = svc_all[shift * nodes_dev + obs_cell // T_DEV]
    eta = jnp.sum(covariates.astype(jnp.float32) * coef_rows, axis=1)
    obs_weight = jnp.exp(eta)
    onehot = (obs_cell[:, None] // T_DEV == jnp.arange(nodes_dev)[None, :]).astype(jnp.bfloat16)
    high = lax.reduce_precision(obs_weight, exponent_bits=8, mantissa_bits=7)
    rest = obs_weight - high
    middle = lax.reduce_precision(rest, exponent_bits=8, mantissa_bits=7)
    low = rest - middle
    slot = owner * T_DEV + obs_cell % T_DEV
    in_slot = slot[:, None] == jnp.arange(space_count * T_DEV)[None, :]
    parts = jnp.concatenate(
        [jnp.where(in_slot, piece[:, None], 0.0) for piece in (high, middle, low)], axis=1
    ).astype(jnp.bfloat16)
    sums = lax.dot_general(
        parts, onehot, (((0,), (0,)), ((), ())), preferred_element_type=jnp.float32
    ).reshape(3, space_count, T_DEV, nodes_dev)
    local_counts = sums[0] + sums[1] + sums[2]
    counted = jnp.sum(
        lax.all_to_all(local_counts, "space", split_axis=0, concat_axis=0, tiled=True), axis=0
    )
    obs_diag = jnp.repeat(counted, PROBES, axis=0).T
    full_diag = base_diag + obs_diag
    local_diag = kappa[:, None] + obs_diag
    applied = (
        scale_space * first_space
        + scale_time * first_time
        + local_diag * rounded.astype(jnp.float32)
    )
    solution = solution + relaxation * (probe_vals - applied) / full_diag
    for sweep in range(ITERS - 1):
        rounded = lax.optimization_barrier(solution.astype(jnp.bfloat16))
        applied = (
            scale_space * spatial(rounded)
            + scale_time * temporal(rounded)
            + local_diag * rounded.astype(jnp.float32)
        )
        solution = solution + relaxation * (probe_vals - applied) / full_diag
    rounded = solution.astype(jnp.bfloat16)
    partial_sums = jnp.stack(
        [
            jnp.sum(probe_vals * spatial(rounded), axis=0),
            jnp.sum(probe_vals * temporal(rounded), axis=0),
        ]
    )
    totals = jnp.sum(
        lax.all_to_all(
            jnp.broadcast_to(partial_sums[None], (space_count,) + partial_sums.shape),
            "space", split_axis=0, concat_axis=0, tiled=True,
        ),
        axis=0,
    )
    grads = totals / (NODES_DEV * space_count)
    return (solution, grads)


def solution(mesh):
    return jax.shard_map(
        shards,
        mesh=mesh,
        in_specs=(
            P("space", "tm"),
            P("space"),
            P("tm"),
            P("tm"),
            P("space", None, None),
            P("space", None, None, None),
            P("space", None),
            P("space"),
            P(("space", "tm"), None),
            P(("space", "tm"), None),
            P(("space", "tm")),
            P("space", None),
        ),
        out_specs=(P("space", "tm"), P(None, "tm")),
        check_vma=False,
    )
```

```python
import jax
import jax.numpy as jnp
from jax import lax
from jax.sharding import PartitionSpec as P

NB_DEV = 8
BLOCK = 128
HALO_B = 2
T_DEV = 4
PROBES = 64
NCOV = 256
OBS_DEV = 2048
ITERS = 4
NODES_DEV = 1024


relaxation = 0.6


def with_halo(array, sides, width):
    for axis, dim in sides:
        peers, length = (lax.axis_size(axis), array.shape[dim])
        up = [(i, (i + 1) % peers) for i in range(peers - 1)]
        down = [(j, i) for i, j in up]
        last = lax.slice_in_dim(array, length - width, length, axis=dim)
        initial = lax.slice_in_dim(array, 0, width, axis=dim)
        before = lax.ppermute(last, axis, up)
        after = lax.ppermute(initial, axis, down)
        array = jnp.concatenate([before, array, after], axis=dim)
    return array


def shards(
    probe_field,
    kappa,
    theta_space,
    theta_time,
    diag_blocks,
    off_blocks,
    block_cols,
    halo_needs,
    covariates,
    obs_owner,
    obs_cell,
    svc_coef,
):
    space_count = lax.axis_size("space")
    columns = probe_field.shape[1]
    width_local = NB_DEV + 2 * HALO_B
    probe_vals = probe_field.astype(jnp.float32)
    eye = jnp.arange(BLOCK)[:, None] == jnp.arange(BLOCK)[None, :]
    sdiag = jnp.sum(jnp.where(eye[None], diag_blocks.astype(jnp.float32), 0.0), axis=2).reshape(
        NODES_DEV
    )
    scale_space = jnp.repeat(theta_space, PROBES)[None, :]
    scale_time = jnp.repeat(theta_time, PROBES)[None, :]
    base_diag = scale_space * sdiag[:, None] + 2.0 * scale_time + kappa[:, None]
    local_ids = jnp.arange(width_local, dtype=jnp.int32)
    picks = (block_cols[:, :, None] == local_ids[None, None, :]).astype(jnp.float32)
    own_pick = (jnp.arange(NB_DEV, dtype=jnp.int32)[:, None] == local_ids[None, :]).astype(
        jnp.float32
    )
    combined = jnp.einsum("bkm,bkij->bimj", picks, off_blocks.astype(jnp.float32))
    combined = combined + jnp.einsum("bm,bij->bimj", own_pick, diag_blocks.astype(jnp.float32))
    combined = combined.astype(jnp.bfloat16).reshape(NODES_DEV, width_local * BLOCK)
    own_part = combined[:, :NODES_DEV]
    lower_part = combined[:, NODES_DEV : NODES_DEV + HALO_B * BLOCK]
    upper_part = combined[:, NODES_DEV + HALO_B * BLOCK :]
    own_t, lower_t, upper_t = own_part.T, lower_part.T, upper_part.T

    space_index = lax.axis_index("space")
    up = [(i, i + 1) for i in range(space_count - 1)]
    down = [(i + 1, i) for i in range(space_count - 1)]
    every_needs = lax.all_to_all(
        jnp.broadcast_to(halo_needs[None], (space_count,) + halo_needs.shape),
        "space", split_axis=0, concat_axis=0, tiled=True,
    )
    space_index = lax.axis_index("space")
    upper_wants = every_needs[jnp.minimum(space_index + 1, space_count - 1), :HALO_B]
    lower_wants = every_needs[jnp.maximum(space_index - 1, 0), HALO_B:]

    def pick_blocks(field, wanted):
        return jnp.concatenate(
            [lax.dynamic_slice_in_dim(field, wanted[j] * BLOCK, BLOCK, axis=0) for j in range(HALO_B)],
            axis=0,
        )

    def spatial(field):
        to_upper = pick_blocks(field, upper_wants)
        to_lower = pick_blocks(field, lower_wants)
        targets = jnp.arange(space_count)[:, None, None]
        outgoing = jnp.where(
            targets == space_index + 1,
            to_upper[None],
            jnp.where(targets == space_index - 1, to_lower[None], jnp.zeros_like(to_upper)[None]),
        )
        incoming = lax.all_to_all(outgoing, "space", split_axis=0, concat_axis=0, tiled=True)
        lower = jnp.where(
            space_index > 0,
            lax.dynamic_index_in_dim(incoming, jnp.maximum(space_index - 1, 0), keepdims=False),
            jnp.zeros_like(to_upper),
        )
        upper = jnp.where(
            space_index < space_count - 1,
            lax.dynamic_index_in_dim(
                incoming, jnp.minimum(space_index + 1, space_count - 1), keepdims=False
            ),
            jnp.zeros_like(to_upper),
        )
        total = jnp.dot(field.T, own_t, preferred_element_type=jnp.float32)
        total = total + jnp.dot(lower.T, lower_t, preferred_element_type=jnp.float32)
        total = total + jnp.dot(upper.T, upper_t, preferred_element_type=jnp.float32)
        return total.T

    def temporal(field):
        arrived = with_halo(field, (("tm", 1),), PROBES)
        return (
            2.0 * field.astype(jnp.float32)
            - arrived[:, :columns].astype(jnp.float32)
            - arrived[:, 2 * PROBES :].astype(jnp.float32)
        )

    solution = relaxation * probe_vals / base_diag
    rounded = lax.optimization_barrier(solution.astype(jnp.bfloat16))
    first_space = spatial(rounded)
    first_time = temporal(rounded)
    nodes_dev = svc_coef.shape[0]
    tables = [svc_coef] + [
        lax.ppermute(svc_coef, "space", [(i, (i + k) % space_count) for i in range(space_count)])
        for k in range(1, space_count)
    ]
    svc_all = jnp.concatenate(tables, axis=0).astype(jnp.float32)
    owner = obs_owner[:, 0]
    shift = (lax.axis_index("space") - owner) % space_count
    coef_rows = svc_all[shift * nodes_dev + obs_cell // T_DEV]
    eta = jnp.sum(covariates.astype(jnp.float32) * coef_rows, axis=1)
    obs_weight = jnp.exp(eta)
    onehot = (obs_cell[:, None] // T_DEV == jnp.arange(nodes_dev)[None, :]).astype(jnp.bfloat16)
    high = lax.reduce_precision(obs_weight, exponent_bits=8, mantissa_bits=7)
    rest = obs_weight - high
    middle = lax.reduce_precision(rest, exponent_bits=8, mantissa_bits=7)
    low = rest - middle
    slot = owner * T_DEV + obs_cell % T_DEV
    in_slot = slot[:, None] == jnp.arange(space_count * T_DEV)[None, :]
    parts = jnp.concatenate(
        [jnp.where(in_slot, piece[:, None], 0.0) for piece in (high, middle, low)], axis=1
    ).astype(jnp.bfloat16)
    sums = lax.dot_general(
        parts, onehot, (((0,), (0,)), ((), ())), preferred_element_type=jnp.float32
    ).reshape(3, space_count, T_DEV, nodes_dev)
    local_counts = sums[0] + sums[1] + sums[2]
    counted = jnp.sum(
        lax.all_to_all(local_counts, "space", split_axis=0, concat_axis=0, tiled=True), axis=0
    )
    obs_diag = jnp.repeat(counted, PROBES, axis=0).T
    full_diag = base_diag + obs_diag
    local_diag = kappa[:, None] + obs_diag
    applied = (
        scale_space * first_space
        + scale_time * first_time
        + local_diag * rounded.astype(jnp.float32)
    )
    solution = solution + relaxation * (probe_vals - applied) / full_diag
    for sweep in range(ITERS - 1):
        rounded = lax.optimization_barrier(solution.astype(jnp.bfloat16))
        applied = (
            scale_space * spatial(rounded)
            + scale_time * temporal(rounded)
            + local_diag * rounded.astype(jnp.float32)
        )
        solution = solution + relaxation * (probe_vals - applied) / full_diag
    rounded = solution.astype(jnp.bfloat16)
    partial_sums = jnp.stack(
        [
            jnp.sum(probe_vals * spatial(rounded), axis=0),
            jnp.sum(probe_vals * temporal(rounded), axis=0),
        ]
    )
    totals = jnp.sum(
        lax.all_to_all(
            jnp.broadcast_to(partial_sums[None], (space_count,) + partial_sums.shape),
            "space", split_axis=0, concat_axis=0, tiled=True,
        ),
        axis=0,
    )
    grads = totals / (NODES_DEV * space_count)
    return (solution, grads)


def solution(mesh):
    return jax.shard_map(
        shards,
        mesh=mesh,
        in_specs=(
            P("space", "tm"),
            P("space"),
            P("tm"),
            P("tm"),
            P("space", None, None),
            P("space", None, None, None),
            P("space", None),
            P("space"),
            P(("space", "tm"), None),
            P(("space", "tm"), None),
            P(("space", "tm")),
            P("space", None),
        ),
        out_specs=(P("space", "tm"), P(None, "tm")),
        check_vma=False,
    )
```

```python
import jax
import jax.numpy as jnp
from jax import lax
from jax.sharding import PartitionSpec as P

NB_DEV = 8
BLOCK = 128
HALO_B = 2
T_DEV = 4
PROBES = 64
NCOV = 256
OBS_DEV = 2048
ITERS = 4
NODES_DEV = 1024


relaxation = 0.6


def with_halo(array, sides, width):
    for axis, dim in sides:
        peers, length = (lax.axis_size(axis), array.shape[dim])
        up = [(i, (i + 1) % peers) for i in range(peers - 1)]
        down = [(j, i) for i, j in up]
        last = lax.slice_in_dim(array, length - width, length, axis=dim)
        initial = lax.slice_in_dim(array, 0, width, axis=dim)
        before = lax.ppermute(last, axis, up)
        after = lax.ppermute(initial, axis, down)
        array = jnp.concatenate([before, array, after], axis=dim)
    return array


def shards(
    probe_field,
    kappa,
    theta_space,
    theta_time,
    diag_blocks,
    off_blocks,
    block_cols,
    halo_needs,
    covariates,
    obs_owner,
    obs_cell,
    svc_coef,
):
    space_count = lax.axis_size("space")
    columns = probe_field.shape[1]
    width_local = NB_DEV + 2 * HALO_B
    probe_vals = probe_field.astype(jnp.float32)
    eye = jnp.arange(BLOCK)[:, None] == jnp.arange(BLOCK)[None, :]
    sdiag = jnp.sum(jnp.where(eye[None], diag_blocks.astype(jnp.float32), 0.0), axis=2).reshape(
        NODES_DEV
    )
    scale_space = jnp.repeat(theta_space, PROBES)[None, :]
    scale_time = jnp.repeat(theta_time, PROBES)[None, :]
    base_diag = scale_space * sdiag[:, None] + 2.0 * scale_time + kappa[:, None]
    local_ids = jnp.arange(width_local, dtype=jnp.int32)
    picks = (block_cols[:, :, None] == local_ids[None, None, :]).astype(jnp.float32)
    own_pick = (jnp.arange(NB_DEV, dtype=jnp.int32)[:, None] == local_ids[None, :]).astype(
        jnp.float32
    )
    combined = jnp.einsum("bkm,bkij->bimj", picks, off_blocks.astype(jnp.float32))
    combined = combined + jnp.einsum("bm,bij->bimj", own_pick, diag_blocks.astype(jnp.float32))
    combined = combined.astype(jnp.bfloat16).reshape(NODES_DEV, width_local * BLOCK)
    own_part = combined[:, :NODES_DEV]
    lower_part = combined[:, NODES_DEV : NODES_DEV + HALO_B * BLOCK]
    upper_part = combined[:, NODES_DEV + HALO_B * BLOCK :]
    own_t, lower_t, upper_t = own_part.T, lower_part.T, upper_part.T

    space_index = lax.axis_index("space")
    up = [(i, i + 1) for i in range(space_count - 1)]
    down = [(i + 1, i) for i in range(space_count - 1)]
    every_needs = lax.all_to_all(
        jnp.broadcast_to(halo_needs[None], (space_count,) + halo_needs.shape),
        "space", split_axis=0, concat_axis=0, tiled=True,
    )
    space_index = lax.axis_index("space")
    upper_wants = every_needs[jnp.minimum(space_index + 1, space_count - 1), :HALO_B]
    lower_wants = every_needs[jnp.maximum(space_index - 1, 0), HALO_B:]

    def pick_blocks(field, wanted):
        return jnp.concatenate(
            [lax.dynamic_slice_in_dim(field, wanted[j] * BLOCK, BLOCK, axis=0) for j in range(HALO_B)],
            axis=0,
        )

    def spatial(field):
        lower = lax.ppermute(pick_blocks(field, upper_wants), "space", up)
        upper = lax.ppermute(pick_blocks(field, lower_wants), "space", down)
        total = jnp.dot(field.T, own_t, preferred_element_type=jnp.float32)
        total = total + jnp.dot(lower.T, lower_t, preferred_element_type=jnp.float32)
        total = total + jnp.dot(upper.T, upper_t, preferred_element_type=jnp.float32)
        return total.T

    def temporal(field):
        arrived = with_halo(field, (("tm", 1),), PROBES)
        return (
            2.0 * field.astype(jnp.float32)
            - arrived[:, :columns].astype(jnp.float32)
            - arrived[:, 2 * PROBES :].astype(jnp.float32)
        )

    solution = relaxation * probe_vals / base_diag
    rounded = solution.astype(jnp.bfloat16)
    first_space = spatial(rounded)
    first_time = temporal(rounded)
    nodes_dev = svc_coef.shape[0]
    tables = [svc_coef] + [
        lax.ppermute(svc_coef, "space", [(i, (i + k) % space_count) for i in range(space_count)])
        for k in range(1, space_count)
    ]
    svc_all = jnp.concatenate(tables, axis=0).astype(jnp.float32)
    owner = obs_owner[:, 0]
    shift = (lax.axis_index("space") - owner) % space_count
    coef_rows = svc_all[shift * nodes_dev + obs_cell // T_DEV]
    eta = jnp.sum(covariates.astype(jnp.float32) * coef_rows, axis=1)
    obs_weight = jnp.exp(eta)
    onehot = (obs_cell[:, None] // T_DEV == jnp.arange(nodes_dev)[None, :]).astype(jnp.bfloat16)
    high = lax.reduce_precision(obs_weight, exponent_bits=8, mantissa_bits=7)
    rest = obs_weight - high
    middle = lax.reduce_precision(rest, exponent_bits=8, mantissa_bits=7)
    low = rest - middle
    slot = owner * T_DEV + obs_cell % T_DEV
    in_slot = slot[:, None] == jnp.arange(space_count * T_DEV)[None, :]
    parts = jnp.concatenate(
        [jnp.where(in_slot, piece[:, None], 0.0) for piece in (high, middle, low)], axis=1
    ).astype(jnp.bfloat16)
    sums = lax.dot_general(
        parts, onehot, (((0,), (0,)), ((), ())), preferred_element_type=jnp.float32
    ).reshape(3, space_count, T_DEV, nodes_dev)
    local_counts = sums[0] + sums[1] + sums[2]
    counted = jnp.sum(
        lax.all_to_all(local_counts, "space", split_axis=0, concat_axis=0, tiled=True), axis=0
    )
    obs_diag = jnp.repeat(counted, PROBES, axis=0).T
    full_diag = base_diag + obs_diag
    local_diag = kappa[:, None] + obs_diag
    applied = (
        scale_space * first_space
        + scale_time * first_time
        + local_diag * rounded.astype(jnp.float32)
    )
    solution = solution + relaxation * (probe_vals - applied) / full_diag
    for sweep in range(ITERS - 1):
        rounded = solution.astype(jnp.bfloat16)
        applied = (
            scale_space * spatial(rounded)
            + scale_time * temporal(rounded)
            + local_diag * rounded.astype(jnp.float32)
        )
        solution = solution + relaxation * (probe_vals - applied) / full_diag
    rounded = solution.astype(jnp.bfloat16)
    partial_sums = jnp.stack(
        [
            jnp.sum(probe_vals * spatial(rounded), axis=0),
            jnp.sum(probe_vals * temporal(rounded), axis=0),
        ]
    )
    totals = jnp.sum(
        lax.all_to_all(
            jnp.broadcast_to(partial_sums[None], (space_count,) + partial_sums.shape),
            "space", split_axis=0, concat_axis=0, tiled=True,
        ),
        axis=0,
    )
    grads = totals / (NODES_DEV * space_count)
    return (solution, grads)


def solution(mesh):
    return jax.shard_map(
        shards,
        mesh=mesh,
        in_specs=(
            P("space", "tm"),
            P("space"),
            P("tm"),
            P("tm"),
            P("space", None, None),
            P("space", None, None, None),
            P("space", None),
            P("space"),
            P(("space", "tm"), None),
            P(("space", "tm"), None),
            P(("space", "tm")),
            P("space", None),
        ),
        out_specs=(P("space", "tm"), P(None, "tm")),
        check_vma=False,
    )
```

```python
import jax
import jax.numpy as jnp
from jax import lax
from jax.sharding import PartitionSpec as P

NB_DEV = 8
BLOCK = 128
HALO_B = 2
T_DEV = 4
PROBES = 64
NCOV = 256
OBS_DEV = 2048
ITERS = 4
NODES_DEV = 1024


relaxation = 0.6


def with_halo(array, sides, width):
    for axis, dim in sides:
        peers, length = (lax.axis_size(axis), array.shape[dim])
        up = [(i, (i + 1) % peers) for i in range(peers - 1)]
        down = [(j, i) for i, j in up]
        last = lax.slice_in_dim(array, length - width, length, axis=dim)
        initial = lax.slice_in_dim(array, 0, width, axis=dim)
        before = lax.ppermute(last, axis, up)
        after = lax.ppermute(initial, axis, down)
        array = jnp.concatenate([before, array, after], axis=dim)
    return array


def shards(
    probe_field,
    kappa,
    theta_space,
    theta_time,
    diag_blocks,
    off_blocks,
    block_cols,
    halo_needs,
    covariates,
    obs_owner,
    obs_cell,
    svc_coef,
):
    space_count = lax.axis_size("space")
    columns = probe_field.shape[1]
    width_local = NB_DEV + 2 * HALO_B
    probe_vals = probe_field.astype(jnp.float32)
    eye = jnp.arange(BLOCK)[:, None] == jnp.arange(BLOCK)[None, :]
    sdiag = jnp.sum(jnp.where(eye[None], diag_blocks.astype(jnp.float32), 0.0), axis=2).reshape(
        NODES_DEV
    )
    scale_space = jnp.repeat(theta_space, PROBES)[None, :]
    scale_time = jnp.repeat(theta_time, PROBES)[None, :]
    base_diag = scale_space * sdiag[:, None] + 2.0 * scale_time + kappa[:, None]
    local_ids = jnp.arange(width_local, dtype=jnp.int32)
    picks = (block_cols[:, :, None] == local_ids[None, None, :]).astype(jnp.float32)
    own_pick = (jnp.arange(NB_DEV, dtype=jnp.int32)[:, None] == local_ids[None, :]).astype(
        jnp.float32
    )
    combined = jnp.einsum("bkm,bkij->bimj", picks, off_blocks.astype(jnp.float32))
    combined = combined + jnp.einsum("bm,bij->bimj", own_pick, diag_blocks.astype(jnp.float32))
    combined = combined.astype(jnp.bfloat16).reshape(NODES_DEV, width_local * BLOCK)
    own_part = combined[:, :NODES_DEV]
    lower_part = combined[:, NODES_DEV : NODES_DEV + HALO_B * BLOCK]
    upper_part = combined[:, NODES_DEV + HALO_B * BLOCK :]
    own_t, lower_t, upper_t = own_part.T, lower_part.T, upper_part.T

    space_index = lax.axis_index("space")
    up = [(i, i + 1) for i in range(space_count - 1)]
    down = [(i + 1, i) for i in range(space_count - 1)]
    every_needs = lax.all_to_all(
        jnp.broadcast_to(halo_needs[None], (space_count,) + halo_needs.shape),
        "space", split_axis=0, concat_axis=0, tiled=True,
    )
    space_index = lax.axis_index("space")
    upper_wants = every_needs[jnp.minimum(space_index + 1, space_count - 1), :HALO_B]
    lower_wants = every_needs[jnp.maximum(space_index - 1, 0), HALO_B:]

    def pick_blocks(field, wanted):
        return jnp.concatenate(
            [lax.dynamic_slice_in_dim(field, wanted[j] * BLOCK, BLOCK, axis=0) for j in range(HALO_B)],
            axis=0,
        )

    def spatial(field):
        lower = lax.ppermute(pick_blocks(field, upper_wants), "space", up)
        upper = lax.ppermute(pick_blocks(field, lower_wants), "space", down)
        total = jnp.dot(field.T, own_t, preferred_element_type=jnp.float32)
        total = total + jnp.dot(lower.T, lower_t, preferred_element_type=jnp.float32)
        total = total + jnp.dot(upper.T, upper_t, preferred_element_type=jnp.float32)
        return total.T, lower

    def temporal(field):
        arrived = with_halo(field, (("tm", 1),), PROBES)
        return (
            2.0 * field.astype(jnp.float32)
            - arrived[:, :columns].astype(jnp.float32)
            - arrived[:, 2 * PROBES :].astype(jnp.float32)
        )

    solution = relaxation * probe_vals / base_diag
    rounded = lax.optimization_barrier(solution.astype(jnp.bfloat16))
    first_space, first_lower = spatial(rounded)
    svc_sent, _ = lax.optimization_barrier((svc_coef, first_lower))
    first_time = temporal(rounded)
    nodes_dev = svc_coef.shape[0]
    tables = [svc_coef] + [
        lax.ppermute(svc_sent, "space", [(i, (i + k) % space_count) for i in range(space_count)])
        for k in range(1, space_count)
    ]
    svc_all = jnp.concatenate(tables, axis=0).astype(jnp.float32)
    owner = obs_owner[:, 0]
    shift = (lax.axis_index("space") - owner) % space_count
    coef_rows = svc_all[shift * nodes_dev + obs_cell // T_DEV]
    eta = jnp.sum(covariates.astype(jnp.float32) * coef_rows, axis=1)
    obs_weight = jnp.exp(eta)
    onehot = (obs_cell[:, None] // T_DEV == jnp.arange(nodes_dev)[None, :]).astype(jnp.bfloat16)
    high = lax.reduce_precision(obs_weight, exponent_bits=8, mantissa_bits=7)
    rest = obs_weight - high
    middle = lax.reduce_precision(rest, exponent_bits=8, mantissa_bits=7)
    low = rest - middle
    slot = owner * T_DEV + obs_cell % T_DEV
    in_slot = slot[:, None] == jnp.arange(space_count * T_DEV)[None, :]
    parts = jnp.concatenate(
        [jnp.where(in_slot, piece[:, None], 0.0) for piece in (high, middle, low)], axis=1
    ).astype(jnp.bfloat16)
    sums = lax.dot_general(
        parts, onehot, (((0,), (0,)), ((), ())), preferred_element_type=jnp.float32
    ).reshape(3, space_count, T_DEV, nodes_dev)
    local_counts = sums[0] + sums[1] + sums[2]
    counted = jnp.sum(
        lax.all_to_all(local_counts, "space", split_axis=0, concat_axis=0, tiled=True), axis=0
    )
    obs_diag = jnp.repeat(counted, PROBES, axis=0).T
    full_diag = base_diag + obs_diag
    local_diag = kappa[:, None] + obs_diag
    applied = (
        scale_space * first_space
        + scale_time * first_time
        + local_diag * rounded.astype(jnp.float32)
    )
    solution = solution + relaxation * (probe_vals - applied) / full_diag
    for sweep in range(ITERS - 1):
        rounded = lax.optimization_barrier(solution.astype(jnp.bfloat16))
        applied = (
            scale_space * spatial(rounded)[0]
            + scale_time * temporal(rounded)
            + local_diag * rounded.astype(jnp.float32)
        )
        solution = solution + relaxation * (probe_vals - applied) / full_diag
    rounded = solution.astype(jnp.bfloat16)
    partial_sums = jnp.stack(
        [
            jnp.sum(probe_vals * spatial(rounded)[0], axis=0),
            jnp.sum(probe_vals * temporal(rounded), axis=0),
        ]
    )
    totals = jnp.sum(
        lax.all_to_all(
            jnp.broadcast_to(partial_sums[None], (space_count,) + partial_sums.shape),
            "space", split_axis=0, concat_axis=0, tiled=True,
        ),
        axis=0,
    )
    grads = totals / (NODES_DEV * space_count)
    return (solution, grads)


def solution(mesh):
    return jax.shard_map(
        shards,
        mesh=mesh,
        in_specs=(
            P("space", "tm"),
            P("space"),
            P("tm"),
            P("tm"),
            P("space", None, None),
            P("space", None, None, None),
            P("space", None),
            P("space"),
            P(("space", "tm"), None),
            P(("space", "tm"), None),
            P(("space", "tm")),
            P("space", None),
        ),
        out_specs=(P("space", "tm"), P(None, "tm")),
        check_vma=False,
    )
```
